128 devices in a mesh: lat: 4 (over z_hi, core), lon: 32 (over z_lo, y, x).
Axes of the slice: x: 4, y: 4, z: 4 (z_hi: 2, z_lo: 2; z = z_hi * 2 + z_lo), core: 2. Of those that a mesh axis runs over, the one named last changes fastest.
Arguments:
- atm_fluxes: bfloat16 [24, 262144], P(None, ('lat', 'lon')), may hold values from -6 to 6
- remap_weights: bfloat16 [128, 256, 128, 128], P(('lat', 'lon')), may hold values from 0 to 0.015625
- source_block: int32 [128, 256], P(('lat', 'lon')), may hold values from 0 to 15
- target_block: int32 [128, 256], P(('lat', 'lon')), may hold values from 0 to 15
- block_count: int32 [128, 128], P(('lat', 'lon')), may hold values from 1 to 2, as said below
- tracers: float32 [6, 16, 64, 4096], P(None, None, 'lat', 'lon'), may hold values from -6 to 6
- east_velocity: float32 [16, 64, 4096], P(None, 'lat', 'lon'), may hold values from -0.3 to 0.3
- north_velocity: float32 [16, 64, 4096], P(None, 'lat', 'lon'), may hold values from -0.3 to 0.3
- land_mask: int32 [64, 4096], P('lat', 'lon'), may hold values 0 or 1
- coupling: float32 [96, 24], replicated, may hold values from -3 to 3
Outputs:
- tracer_out: float32 [6, 16, 64, 4096], P(None, None, 'lat', 'lon')
The draws below stay inside these ranges and needn't reach their ends.
Inputs may be any that keep to these rules, and one draw needn't show every extreme that they name: Slots 0 to block_count - 1 of a source and tile carry data; in every draw one tile receives all 2 slots from every source.
All inputs are finite; a program needn't handle non-finite values. No bound on the sum of `land_mask` on one device may be relied on, other than what follows from the above.
Results may differ from the reference program's by a relative error of at most 0.0003.
Values sent between devices are 32-bit elements; how exact they have to be, the bound alone decides.
No kernel may reach another device: no remote copies, remote signals or barrier semaphores. Data moves between devices by JAX's collectives and lax.ppermute only.
A program may use at most 128 MiB of HBM per device.

```python
import jax
import jax.numpy as jnp
from jax import lax

NFLX = 24
NTR = 6
BLOCK = 128
LEV = 16
NSUB = 4
SLOTS = 2
CLAT = 16
ABLK = 16
TILES = 128
NLAT = 64
NLON = 4096
ACELLS = 262144
N_LAT = 4
N_LON = 32


def draw_block_count(key, part):
    base_key = jax.random.fold_in(key, 11)
    full_key = jax.random.fold_in(key, 23)
    base = jax.random.randint(base_key, (TILES, TILES), 1, SLOTS + 1, dtype=jnp.int32)
    full_tile = jax.random.randint(full_key, (), 0, TILES, dtype=jnp.int32)
    columns = jnp.arange(TILES, dtype=jnp.int32)[None, :]
    return jnp.where(columns == full_tile, jnp.int32(SLOTS), base)


def touch_ends(entries, key, least, top_value):
    dims = entries.shape
    spot = [jax.random.randint(jax.random.fold_in(key, axis), (), 0, dims[axis]) for axis in range(len(dims))]
    entries = entries.at[tuple(spot)].set(least)
    longest = dims.index(max(dims))
    spot[longest] = (spot[longest] + 1) % dims[longest]
    return entries.at[tuple(spot)].set(top_value)


def steps_of(own_key, dims, cuts, low, top_value):
    level = 1.0
    for axis_at, blocks in cuts:
        heights = jax.random.uniform(jax.random.fold_in(jax.random.fold_in(own_key, 6), axis_at), (blocks,), jnp.float32, low / len(cuts), top_value / len(cuts))
        level = level * jnp.repeat(jnp.exp(heights), dims[axis_at] // blocks).reshape((-1,) + (1,) * (len(dims) - 1 - axis_at))
    return level


def centred(stream_key, dims, deviation, limit, pieces=(), kind=jnp.bfloat16):
    drawn = jax.random.normal(stream_key, dims, jnp.float32) * deviation
    if len(pieces) > 0:
        drawn = steps_of(stream_key, dims, pieces, -0.22, 0.18) * drawn
    return jnp.clip(drawn, min=-limit, max=limit).astype(kind)


def setup_inputs(seed: int = 0) -> dict:
    key_of = jax.random.split(jax.random.key(seed), 11)
    atm_fluxes = centred(key_of[0], (NFLX, ACELLS), 1.0, 6.0, ((1, 128),))
    remap_weights = jnp.clip(0.015625 * jax.random.uniform(key_of[1], (TILES, TILES * SLOTS, BLOCK, BLOCK), jnp.float32) ** steps_of(key_of[1], (TILES, TILES * SLOTS, BLOCK, BLOCK), ((0, 128),), -0.2, 0.2), 0.0, 0.015625).astype(jnp.bfloat16)
    source_block = touch_ends(jax.random.randint(key_of[2], (TILES, TILES * SLOTS), 0, ABLK), jax.random.fold_in(key_of[2], 1), 0, ABLK - 1).astype(jnp.int32)
    target_block = touch_ends(jax.random.randint(key_of[3], (TILES, TILES * SLOTS), 0, CLAT), jax.random.fold_in(key_of[3], 1), 0, CLAT - 1).astype(jnp.int32)
    block_count = draw_block_count(jax.random.fold_in(key_of[10], 71), 0)
    tracers = centred(key_of[5], (NTR, LEV, NLAT, NLON), 1.0, 6.0, ((2, 4), (3, 32)), jnp.float32)
    east_velocity = jnp.clip(jax.random.uniform(key_of[6], (LEV, NLAT, NLON), jnp.float32, -0.3, 0.3) * steps_of(key_of[6], (LEV, NLAT, NLON), ((1, 4), (2, 32)), -0.4, 0.0), -0.3, 0.3)
    north_velocity = jnp.clip(jax.random.uniform(key_of[7], (LEV, NLAT, NLON), jnp.float32, -0.3, 0.3) * steps_of(key_of[7], (LEV, NLAT, NLON), ((1, 4), (2, 32)), -0.4, 0.0), -0.3, 0.3)
    land_mask = touch_ends((jax.random.randint(key_of[8], (NLAT, NLON), 0, 10) < 7).astype(jnp.int32), jax.random.fold_in(key_of[8], 1), 0, 1)
    coupling = centred(key_of[9], (NTR * LEV, NFLX), 0.5, 3.0, (), jnp.float32)
    return {"atm_fluxes": atm_fluxes, "remap_weights": remap_weights, "source_block": source_block, "target_block": target_block, "block_count": block_count, "tracers": tracers, "east_velocity": east_velocity, "north_velocity": north_velocity, "land_mask": land_mask, "coupling": coupling}


diffusion_number = 0.2


def advect(tracer_now, east_speed, north_speed, sea_mask):
    mask_east = sea_mask[:, :-1] * sea_mask[:, 1:]
    east_flow = mask_east * (east_speed[:, :, :-1] * (tracer_now[..., :-1] + tracer_now[..., 1:]) * 0.5 - diffusion_number * (tracer_now[..., 1:] - tracer_now[..., :-1]))
    mask_north = sea_mask[:-1, :] * sea_mask[1:, :]
    north_flow = mask_north * (north_speed[:, :-1, :] * (tracer_now[..., :-1, :] + tracer_now[..., 1:, :]) * 0.5 - diffusion_number * (tracer_now[..., 1:, :] - tracer_now[..., :-1, :]))
    inner = tracer_now[..., 1:-1, 1:-1]
    return inner + east_flow[..., 1:-1, :-1] - east_flow[..., 1:-1, 1:] + north_flow[..., :-1, 1:-1] - north_flow[..., 1:, 1:-1]


def extend(field):
    widths = [(0, 0)] * (field.ndim - 2) + [(1, 1), (0, 0)]
    padded = jnp.pad(field, widths)
    return jnp.concatenate([padded[..., -1:], padded, padded[..., :1]], axis=-1)


def reference(atm_fluxes, remap_weights, source_block, target_block, block_count, tracers, east_velocity, north_velocity, land_mask, coupling):
    atm_blocks = atm_fluxes.astype(jnp.float32).reshape(NFLX, TILES, ABLK, BLOCK)
    slot_ids = jnp.arange(TILES * SLOTS, dtype=jnp.int32)
    dest_tile = slot_ids // SLOTS
    is_live = (slot_ids % SLOTS)[None, :] < jnp.repeat(block_count, SLOTS, axis=1)

    def add_source(source_dev, totals):
        local = lax.dynamic_index_in_dim(atm_blocks, source_dev, 1, keepdims=False)
        chosen = jnp.take(local, source_block[source_dev], axis=1)
        weights = remap_weights[source_dev].astype(jnp.float32)
        partial_value = jnp.einsum("fsb,sbc->sfc", chosen, weights, precision=lax.Precision.HIGHEST)
        partial_value = jnp.where(is_live[source_dev][:, None, None], partial_value, jnp.float32(0.0))
        return totals.at[dest_tile, target_block[source_dev]].add(partial_value)

    totals = lax.fori_loop(0, TILES, add_source, jnp.zeros((TILES, CLAT, NFLX, BLOCK), jnp.float32))
    ocean_flux = totals.reshape(N_LAT, N_LON, CLAT, NFLX, BLOCK).transpose(3, 0, 2, 1, 4).reshape(NFLX, NLAT, NLON)
    source = jnp.einsum("pf,fij->pij", coupling, ocean_flux, precision=lax.Precision.HIGHEST).reshape(NTR, LEV, NLAT, NLON)
    sea_mask = land_mask.astype(jnp.float32)
    mask_wide = extend(sea_mask)
    east_wide = extend(east_velocity)
    north_wide = extend(north_velocity)
    tracer_now = tracers
    for substep in range(NSUB):
        tracer_now = advect(extend(tracer_now), east_wide, north_wide, mask_wide)
    return tracer_now + sea_mask * source
```

```python
import jax
import jax.numpy as jnp
from jax import lax
from jax.sharding import PartitionSpec as P

NSUB = 4


diffusion_number = 0.2


def shifted_pairs(count, step, wrap):
    pairs = []
    for i in range(count):
        j = i + step
        if 0 <= j < count:
            pairs.append((i, j))
        elif wrap:
            pairs.append((i, j % count))
    return pairs


def with_halo(block, width):
    lon_count = lax.axis_size("lon")
    lat_count = lax.axis_size("lat")
    west = lax.ppermute(block[..., -width:], "lon", shifted_pairs(lon_count, 1, True))
    east = lax.ppermute(block[..., :width], "lon", shifted_pairs(lon_count, -1, True))
    block = jnp.concatenate([west, block, east], axis=-1)
    south = lax.ppermute(block[..., -width:, :], "lat", shifted_pairs(lat_count, 1, False))
    north = lax.ppermute(block[..., :width, :], "lat", shifted_pairs(lat_count, -1, False))
    return jnp.concatenate([south, block, north], axis=-2)


def advect(tracer_now, east_speed, north_speed, sea_mask):
    mask_east = sea_mask[:, :-1] * sea_mask[:, 1:]
    east_flow = mask_east * (
        east_speed[:, :, :-1] * (tracer_now[..., :-1] + tracer_now[..., 1:]) * 0.5
        - diffusion_number * (tracer_now[..., 1:] - tracer_now[..., :-1])
    )
    mask_north = sea_mask[:-1, :] * sea_mask[1:, :]
    north_flow = mask_north * (
        north_speed[:, :-1, :] * (tracer_now[..., :-1, :] + tracer_now[..., 1:, :]) * 0.5
        - diffusion_number * (tracer_now[..., 1:, :] - tracer_now[..., :-1, :])
    )
    inner = tracer_now[..., 1:-1, 1:-1]
    return (
        inner
        + east_flow[..., 1:-1, :-1]
        - east_flow[..., 1:-1, 1:]
        + north_flow[..., :-1, 1:-1]
        - north_flow[..., 1:, 1:-1]
    )


def per_device(
    atm_fluxes,
    remap_weights,
    source_block,
    target_block,
    block_count,
    tracers,
    east_velocity,
    north_velocity,
    land_mask,
    coupling,
):
    field_count, cell_count = atm_fluxes.shape
    block_cells = remap_weights.shape[-1]
    tile_count = block_count.shape[1]
    slot_count = source_block.shape[1] // tile_count
    tracer_count, level_count, lat_rows, lon_cols = tracers.shape

    atm_blocks = atm_fluxes.reshape(field_count, cell_count // block_cells, block_cells)
    chosen = jnp.take(atm_blocks, source_block[0], axis=1)
    partials = jnp.einsum(
        "fsb,sbc->sfc", chosen, remap_weights[0], preferred_element_type=jnp.float32
    )
    slot_ids = jnp.arange(tile_count * slot_count, dtype=jnp.int32)
    is_live = slot_ids % slot_count < jnp.repeat(block_count[0], slot_count)
    partials = jnp.where(is_live[:, None, None], partials, jnp.float32(0.0))
    targets = jnp.where(is_live, target_block[0], -1).astype(jnp.float32)
    arrived = lax.all_to_all(
        partials.reshape(tile_count, slot_count * field_count, block_cells),
        ("lat", "lon"),
        split_axis=0,
        concat_axis=0,
        tiled=True,
    )
    landed = lax.all_to_all(
        targets.reshape(tile_count, slot_count),
        ("lat", "lon"),
        split_axis=0,
        concat_axis=0,
        tiled=True,
    )

    sea_here = land_mask.astype(jnp.float32)
    planes = tracer_count * level_count
    stacked = jnp.concatenate(
        [
            tracers.reshape(planes, lat_rows, lon_cols),
            east_velocity,
            north_velocity,
            sea_here[None],
        ],
        axis=0,
    )
    wide = with_halo(stacked, NSUB)
    tracer_now = wide[:planes].reshape(tracer_count, level_count, lat_rows + 2 * NSUB, lon_cols + 2 * NSUB)
    east_wide = wide[planes : planes + level_count]
    north_wide = wide[planes + level_count : planes + 2 * level_count]
    mask_wide = wide[-1]
    for substep in range(NSUB):
        cut = substep
        end_r = lat_rows + 2 * NSUB - cut
        end_c = lon_cols + 2 * NSUB - cut
        tracer_now = advect(
            tracer_now,
            east_wide[:, cut:end_r, cut:end_c],
            north_wide[:, cut:end_r, cut:end_c],
            mask_wide[cut:end_r, cut:end_c],
        )

    arrived = arrived.reshape(tile_count * slot_count, field_count, block_cells)
    landed = landed.reshape(tile_count * slot_count)
    chooser = (landed[None, :] == jnp.arange(lat_rows, dtype=jnp.float32)[:, None]).astype(
        jnp.float32
    )
    ocean_flux = jnp.einsum(
        "rk,kfc->rfc", chooser, arrived, precision=lax.Precision.HIGHEST,
        preferred_element_type=jnp.float32,
    )
    source = jnp.einsum(
        "pf,ifj->pij", coupling, ocean_flux, precision=lax.Precision.HIGHEST
    ).reshape(tracer_count, level_count, lat_rows, lon_cols)
    return tracer_now + sea_here * source


def solution(mesh):
    placed = (
        P(None, ("lat", "lon")),
        P(("lat", "lon"), None, None, None),
        P(("lat", "lon"), None),
        P(("lat", "lon"), None),
        P(("lat", "lon"), None),
        P(None, None, "lat", "lon"),
        P(None, "lat", "lon"),
        P(None, "lat", "lon"),
        P("lat", "lon"),
        P(),
    )
    return jax.shard_map(
        per_device,
        mesh=mesh,
        in_specs=placed,
        out_specs=P(None, None, "lat", "lon"),
        check_vma=False,
    )
```

```python
import jax
import jax.numpy as jnp
from jax import lax
from jax.sharding import PartitionSpec as P

NSUB = 4


diffusion_number = 0.2


def shifted_pairs(count, step, wrap):
    pairs = []
    for i in range(count):
        j = i + step
        if 0 <= j < count:
            pairs.append((i, j))
        elif wrap:
            pairs.append((i, j % count))
    return pairs


def with_halo(block, width):
    lon_count = lax.axis_size("lon")
    lat_count = lax.axis_size("lat")
    west = lax.ppermute(block[..., -width:], "lon", shifted_pairs(lon_count, 1, True))
    east = lax.ppermute(block[..., :width], "lon", shifted_pairs(lon_count, -1, True))
    block = jnp.concatenate([west, block, east], axis=-1)
    south = lax.ppermute(block[..., -width:, :], "lat", shifted_pairs(lat_count, 1, False))
    north = lax.ppermute(block[..., :width, :], "lat", shifted_pairs(lat_count, -1, False))
    return jnp.concatenate([south, block, north], axis=-2)


def advect(tracer_now, east_speed, north_speed, sea_mask):
    mask_east = sea_mask[:, :-1] * sea_mask[:, 1:]
    east_flow = mask_east * (
        east_speed[:, :, :-1] * (tracer_now[..., :-1] + tracer_now[..., 1:]) * 0.5
        - diffusion_number * (tracer_now[..., 1:] - tracer_now[..., :-1])
    )
    mask_north = sea_mask[:-1, :] * sea_mask[1:, :]
    north_flow = mask_north * (
        north_speed[:, :-1, :] * (tracer_now[..., :-1, :] + tracer_now[..., 1:, :]) * 0.5
        - diffusion_number * (tracer_now[..., 1:, :] - tracer_now[..., :-1, :])
    )
    inner = tracer_now[..., 1:-1, 1:-1]
    return (
        inner
        + east_flow[..., 1:-1, :-1]
        - east_flow[..., 1:-1, 1:]
        + north_flow[..., :-1, 1:-1]
        - north_flow[..., 1:, 1:-1]
    )


def per_device(
    atm_fluxes,
    remap_weights,
    source_block,
    target_block,
    block_count,
    tracers,
    east_velocity,
    north_velocity,
    land_mask,
    coupling,
):
    field_count, cell_count = atm_fluxes.shape
    block_cells = remap_weights.shape[-1]
    tile_count = block_count.shape[1]
    slot_count = source_block.shape[1] // tile_count
    tracer_count, level_count, lat_rows, lon_cols = tracers.shape

    atm_blocks = atm_fluxes.reshape(field_count, cell_count // block_cells, block_cells)
    chosen = jnp.take(atm_blocks, source_block[0], axis=1)
    partials = jnp.einsum(
        "fsb,sbc->sfc", chosen, remap_weights[0], preferred_element_type=jnp.float32
    )
    slot_ids = jnp.arange(tile_count * slot_count, dtype=jnp.int32)
    is_live = slot_ids % slot_count < jnp.repeat(block_count[0], slot_count)
    partials = jnp.where(is_live[:, None, None], partials, jnp.float32(0.0))
    targets = jnp.where(is_live, target_block[0], -1).astype(jnp.float32)
    sent = partials.reshape(tile_count, slot_count * field_count, block_cells)
    sent, tracers, east_velocity, north_velocity, land_mask = lax.optimization_barrier(
        (sent, tracers, east_velocity, north_velocity, land_mask)
    )
    arrived = lax.all_to_all(sent, ("lat", "lon"), split_axis=0, concat_axis=0, tiled=True)
    every_target = lax.all_gather(targets, ("lat", "lon"))
    me = lax.axis_index("lat") * lax.axis_size("lon") + lax.axis_index("lon")
    landed = lax.dynamic_slice_in_dim(every_target, me * slot_count, slot_count, axis=1)

    sea_here = land_mask.astype(jnp.float32)
    planes = tracer_count * level_count
    stacked = jnp.concatenate(
        [
            tracers.reshape(planes, lat_rows, lon_cols),
            east_velocity,
            north_velocity,
            sea_here[None],
        ],
        axis=0,
    )
    wide = with_halo(stacked, NSUB)
    tracer_now = wide[:planes].reshape(tracer_count, level_count, lat_rows + 2 * NSUB, lon_cols + 2 * NSUB)
    east_wide = wide[planes : planes + level_count]
    north_wide = wide[planes + level_count : planes + 2 * level_count]
    mask_wide = wide[-1]
    for substep in range(NSUB):
        cut = substep
        end_r = lat_rows + 2 * NSUB - cut
        end_c = lon_cols + 2 * NSUB - cut
        tracer_now = advect(
            tracer_now,
            east_wide[:, cut:end_r, cut:end_c],
            north_wide[:, cut:end_r, cut:end_c],
            mask_wide[cut:end_r, cut:end_c],
        )

    arrived = arrived.reshape(tile_count * slot_count, field_count, block_cells)
    landed = landed.reshape(tile_count * slot_count)
    chooser = (landed[None, :] == jnp.arange(lat_rows, dtype=jnp.float32)[:, None]).astype(
        jnp.float32
    )
    ocean_flux = jnp.einsum(
        "rk,kfc->rfc", chooser, arrived, precision=lax.Precision.HIGHEST,
        preferred_element_type=jnp.float32,
    )
    source = jnp.einsum(
        "pf,ifj->pij", coupling, ocean_flux, precision=lax.Precision.HIGHEST
    ).reshape(tracer_count, level_count, lat_rows, lon_cols)
    return tracer_now + sea_here * source


def solution(mesh):
    placed = (
        P(None, ("lat", "lon")),
        P(("lat", "lon"), None, None, None),
        P(("lat", "lon"), None),
        P(("lat", "lon"), None),
        P(("lat", "lon"), None),
        P(None, None, "lat", "lon"),
        P(None, "lat", "lon"),
        P(None, "lat", "lon"),
        P("lat", "lon"),
        P(),
    )
    return jax.shard_map(
        per_device,
        mesh=mesh,
        in_specs=placed,
        out_specs=P(None, None, "lat", "lon"),
        check_vma=False,
    )
```

```python
import jax
import jax.numpy as jnp
from jax import lax
from jax.sharding import PartitionSpec as P


NSUB = 4


diffusion_number = 0.2


def shifted_pairs(count, step, wrap):
    pairs = []
    for i in range(count):
        j = i + step
        if 0 <= j < count:
            pairs.append((i, j))
        elif wrap:
            pairs.append((i, j % count))
    return pairs


def with_halo(block, width):
    lon_count = lax.axis_size("lon")
    lat_count = lax.axis_size("lat")
    west = lax.ppermute(block[..., -width:], "lon", shifted_pairs(lon_count, 1, True))
    east = lax.ppermute(block[..., :width], "lon", shifted_pairs(lon_count, -1, True))
    block = jnp.concatenate([west, block, east], axis=-1)
    south = lax.ppermute(block[..., -width:, :], "lat", shifted_pairs(lat_count, 1, False))
    north = lax.ppermute(block[..., :width, :], "lat", shifted_pairs(lat_count, -1, False))
    return jnp.concatenate([south, block, north], axis=-2)


def advect(tracer_now, east_speed, north_speed, sea_mask):
    mask_east = sea_mask[:, :-1] * sea_mask[:, 1:]
    east_flow = mask_east * (
        east_speed[:, :, :-1] * (tracer_now[..., :-1] + tracer_now[..., 1:]) * 0.5
        - diffusion_number * (tracer_now[..., 1:] - tracer_now[..., :-1])
    )
    mask_north = sea_mask[:-1, :] * sea_mask[1:, :]
    north_flow = mask_north * (
        north_speed[:, :-1, :] * (tracer_now[..., :-1, :] + tracer_now[..., 1:, :]) * 0.5
        - diffusion_number * (tracer_now[..., 1:, :] - tracer_now[..., :-1, :])
    )
    inner = tracer_now[..., 1:-1, 1:-1]
    return (
        inner
        + east_flow[..., 1:-1, :-1]
        - east_flow[..., 1:-1, 1:]
        + north_flow[..., :-1, 1:-1]
        - north_flow[..., 1:, 1:-1]
    )


def coupled_step(
    atm_fluxes,
    remap_weights,
    source_block,
    target_block,
    block_count,
    tracers,
    east_velocity,
    north_velocity,
    land_mask,
    coupling,
):
    field_count, cell_count = atm_fluxes.shape
    block_cells = remap_weights.shape[-1]
    tile_count = block_count.shape[1]
    slot_count = source_block.shape[1] // tile_count
    tracer_count, level_count, lat_rows, lon_cols = tracers.shape

    atm_blocks = atm_fluxes.reshape(field_count, cell_count // block_cells, block_cells)
    chosen = jnp.take(atm_blocks, source_block[0], axis=1)
    partials = jnp.einsum(
        "fsb,sbc->sfc", chosen, remap_weights[0], preferred_element_type=jnp.float32
    )
    slot_ids = jnp.arange(tile_count * slot_count, dtype=jnp.int32)
    is_live = slot_ids % slot_count < jnp.repeat(block_count[0], slot_count)
    partials = jnp.where(is_live[:, None, None], partials, jnp.float32(0.0))
    targets = jnp.where(is_live, target_block[0], -1).astype(jnp.float32)
    sent = partials.reshape(tile_count, slot_count * field_count, block_cells)
    sent, tracers, east_velocity, north_velocity, land_mask = lax.optimization_barrier(
        (sent, tracers, east_velocity, north_velocity, land_mask)
    )
    arrived = lax.all_to_all(sent, ("lat", "lon"), split_axis=0, concat_axis=0, tiled=True)
    me = lax.axis_index("lat") * lax.axis_size("lon") + lax.axis_index("lon")
    spread = jnp.where(
        jnp.arange(tile_count)[None, :, None] == me,
        targets.reshape(tile_count, 1, slot_count),
        jnp.float32(0.0),
    )
    landed = lax.psum_scatter(spread, ("lat", "lon"), scatter_dimension=0, tiled=True)

    sea_here = land_mask.astype(jnp.float32)
    planes = tracer_count * level_count
    stacked = jnp.concatenate(
        [
            tracers.reshape(planes, lat_rows, lon_cols),
            east_velocity,
            north_velocity,
            sea_here[None],
        ],
        axis=0,
    )
    wide = with_halo(stacked, NSUB)
    tracer_now = wide[:planes].reshape(tracer_count, level_count, lat_rows + 2 * NSUB, lon_cols + 2 * NSUB)
    east_wide = wide[planes : planes + level_count]
    north_wide = wide[planes + level_count : planes + 2 * level_count]
    mask_wide = wide[-1]
    for substep in range(NSUB):
        cut = substep
        end_r = lat_rows + 2 * NSUB - cut
        end_c = lon_cols + 2 * NSUB - cut
        tracer_now = advect(
            tracer_now,
            east_wide[:, cut:end_r, cut:end_c],
            north_wide[:, cut:end_r, cut:end_c],
            mask_wide[cut:end_r, cut:end_c],
        )

    arrived = arrived.reshape(tile_count * slot_count, field_count, block_cells)
    landed = landed.reshape(tile_count * slot_count)
    chooser = (landed[None, :] == jnp.arange(lat_rows, dtype=jnp.float32)[:, None]).astype(
        jnp.float32
    )
    ocean_flux = jnp.einsum(
        "rk,kfc->rfc", chooser, arrived, precision=lax.Precision.HIGHEST,
        preferred_element_type=jnp.float32,
    )
    source = jnp.einsum(
        "pf,ifj->pij", coupling, ocean_flux, precision=lax.Precision.HIGHEST
    ).reshape(tracer_count, level_count, lat_rows, lon_cols)
    return tracer_now + sea_here * source


def solution(mesh):
    placed = (
        P(None, ("lat", "lon")),
        P(("lat", "lon"), None, None, None),
        P(("lat", "lon"), None),
        P(("lat", "lon"), None),
        P(("lat", "lon"), None),
        P(None, None, "lat", "lon"),
        P(None, "lat", "lon"),
        P(None, "lat", "lon"),
        P("lat", "lon"),
        P(),
    )
    return jax.shard_map(
        coupled_step,
        mesh=mesh,
        in_specs=placed,
        out_specs=P(None, None, "lat", "lon"),
        check_vma=False,
    )
```

```python
import jax
import jax.numpy as jnp
from jax import lax
from jax.sharding import PartitionSpec as P


NSUB = 4


diffusion_number = 0.2


def neighbour_pairs(lat_count, lon_count, dlat, dlon):
    pairs = []
    for a in range(lat_count):
        for o in range(lon_count):
            b = a + dlat
            if 0 <= b < lat_count:
                pairs.append((a * lon_count + o, b * lon_count + (o + dlon) % lon_count))
    return pairs


def with_halo(block, width):
    lat_count = lax.axis_size("lat")
    lon_count = lax.axis_size("lon")
    rows, cols = block.shape[-2:]
    row_part = {-1: slice(0, width), 0: slice(None), 1: slice(rows - width, rows)}
    col_part = {-1: slice(0, width), 0: slice(None), 1: slice(cols - width, cols)}
    got = {}
    for dlat in (-1, 0, 1):
        for dlon in (-1, 0, 1):
            if dlat == 0 and dlon == 0:
                continue
            got[dlat, dlon] = lax.ppermute(
                block[..., row_part[dlat], col_part[dlon]],
                ("lat", "lon"),
                neighbour_pairs(lat_count, lon_count, dlat, dlon),
            )
    south = jnp.concatenate([got[1, 1], got[1, 0], got[1, -1]], axis=-1)
    middle = jnp.concatenate([got[0, 1], block, got[0, -1]], axis=-1)
    north = jnp.concatenate([got[-1, 1], got[-1, 0], got[-1, -1]], axis=-1)
    return jnp.concatenate([south, middle, north], axis=-2)


def advect(tracer_now, east_speed, north_speed, sea_mask):
    mask_east = sea_mask[:, :-1] * sea_mask[:, 1:]
    east_flow = mask_east * (
        east_speed[:, :, :-1] * (tracer_now[..., :-1] + tracer_now[..., 1:]) * 0.5
        - diffusion_number * (tracer_now[..., 1:] - tracer_now[..., :-1])
    )
    mask_north = sea_mask[:-1, :] * sea_mask[1:, :]
    north_flow = mask_north * (
        north_speed[:, :-1, :] * (tracer_now[..., :-1, :] + tracer_now[..., 1:, :]) * 0.5
        - diffusion_number * (tracer_now[..., 1:, :] - tracer_now[..., :-1, :])
    )
    inner = tracer_now[..., 1:-1, 1:-1]
    return (
        inner
        + east_flow[..., 1:-1, :-1]
        - east_flow[..., 1:-1, 1:]
        + north_flow[..., :-1, 1:-1]
        - north_flow[..., 1:, 1:-1]
    )


def coupled_step(
    atm_fluxes,
    remap_weights,
    source_block,
    target_block,
    block_count,
    tracers,
    east_velocity,
    north_velocity,
    land_mask,
    coupling,
):
    field_count, cell_count = atm_fluxes.shape
    block_cells = remap_weights.shape[-1]
    tile_count = block_count.shape[1]
    slot_count = source_block.shape[1] // tile_count
    tracer_count, level_count, lat_rows, lon_cols = tracers.shape

    atm_blocks = atm_fluxes.reshape(field_count, cell_count // block_cells, block_cells)
    chosen = jnp.take(atm_blocks, source_block[0], axis=1)
    partials = jnp.einsum(
        "fsb,sbc->sfc", chosen, remap_weights[0], preferred_element_type=jnp.float32
    )
    slot_ids = jnp.arange(tile_count * slot_count, dtype=jnp.int32)
    is_live = slot_ids % slot_count < jnp.repeat(block_count[0], slot_count)
    partials = jnp.where(is_live[:, None, None], partials, jnp.float32(0.0))
    targets = jnp.where(is_live, target_block[0], -1).astype(jnp.float32)
    sent = partials.reshape(tile_count, slot_count * field_count, block_cells)
    arrived = lax.all_to_all(sent, ("lat", "lon"), split_axis=0, concat_axis=0, tiled=True)
    landed = lax.all_to_all(
        targets.reshape(tile_count, slot_count),
        ("lat", "lon"),
        split_axis=0,
        concat_axis=0,
        tiled=True,
    )

    sea_here = land_mask.astype(jnp.float32)
    planes = tracer_count * level_count
    stacked = jnp.concatenate(
        [
            tracers.reshape(planes, lat_rows, lon_cols),
            east_velocity,
            north_velocity,
            sea_here[None],
        ],
        axis=0,
    )
    wide = with_halo(stacked, NSUB)
    tracer_now = wide[:planes].reshape(tracer_count, level_count, lat_rows + 2 * NSUB, lon_cols + 2 * NSUB)
    east_wide = wide[planes : planes + level_count]
    north_wide = wide[planes + level_count : planes + 2 * level_count]
    mask_wide = wide[-1]
    for substep in range(NSUB):
        cut = substep
        end_r = lat_rows + 2 * NSUB - cut
        end_c = lon_cols + 2 * NSUB - cut
        tracer_now = advect(
            tracer_now,
            east_wide[:, cut:end_r, cut:end_c],
            north_wide[:, cut:end_r, cut:end_c],
            mask_wide[cut:end_r, cut:end_c],
        )

    arrived = arrived.reshape(tile_count * slot_count, field_count, block_cells)
    landed = landed.reshape(tile_count * slot_count)
    chooser = (landed[None, :] == jnp.arange(lat_rows, dtype=jnp.float32)[:, None]).astype(
        jnp.float32
    )
    ocean_flux = jnp.einsum(
        "rk,kfc->rfc", chooser, arrived, precision=lax.Precision.HIGHEST,
        preferred_element_type=jnp.float32,
    )
    source = jnp.einsum(
        "pf,ifj->pij", coupling, ocean_flux, precision=lax.Precision.HIGHEST
    ).reshape(tracer_count, level_count, lat_rows, lon_cols)
    return tracer_now + sea_here * source


def solution(mesh):
    placed = (
        P(None, ("lat", "lon")),
        P(("lat", "lon"), None, None, None),
        P(("lat", "lon"), None),
        P(("lat", "lon"), None),
        P(("lat", "lon"), None),
        P(None, None, "lat", "lon"),
        P(None, "lat", "lon"),
        P(None, "lat", "lon"),
        P("lat", "lon"),
        P(),
    )
    return jax.shard_map(
        coupled_step,
        mesh=mesh,
        in_specs=placed,
        out_specs=P(None, None, "lat", "lon"),
        check_vma=False,
    )
```

```python
import jax
import jax.numpy as jnp
from jax import lax
from jax.sharding import PartitionSpec as P


NSUB = 4


diffusion_number = 0.2


def shifted_pairs(count, step, wrap):
    pairs = []
    for i in range(count):
        j = i + step
        if 0 <= j < count:
            pairs.append((i, j))
        elif wrap:
            pairs.append((i, j % count))
    return pairs


def with_halo(block, width):
    lon_count = lax.axis_size("lon")
    lat_count = lax.axis_size("lat")
    west = lax.ppermute(block[..., -width:], "lon", shifted_pairs(lon_count, 1, True))
    east = lax.ppermute(block[..., :width], "lon", shifted_pairs(lon_count, -1, True))
    block = jnp.concatenate([west, block, east], axis=-1)
    south = lax.ppermute(block[..., -width:, :], "lat", shifted_pairs(lat_count, 1, False))
    north = lax.ppermute(block[..., :width, :], "lat", shifted_pairs(lat_count, -1, False))
    return jnp.concatenate([south, block, north], axis=-2)


def advect(tracer_now, east_speed, north_speed, sea_mask):
    mask_east = sea_mask[:, :-1] * sea_mask[:, 1:]
    east_flow = mask_east * (
        east_speed[:, :, :-1] * (tracer_now[..., :-1] + tracer_now[..., 1:]) * 0.5
        - diffusion_number * (tracer_now[..., 1:] - tracer_now[..., :-1])
    )
    mask_north = sea_mask[:-1, :] * sea_mask[1:, :]
    north_flow = mask_north * (
        north_speed[:, :-1, :] * (tracer_now[..., :-1, :] + tracer_now[..., 1:, :]) * 0.5
        - diffusion_number * (tracer_now[..., 1:, :] - tracer_now[..., :-1, :])
    )
    inner = tracer_now[..., 1:-1, 1:-1]
    return (
        inner
        + east_flow[..., 1:-1, :-1]
        - east_flow[..., 1:-1, 1:]
        + north_flow[..., :-1, 1:-1]
        - north_flow[..., 1:, 1:-1]
    )


def coupled_step(
    atm_fluxes,
    remap_weights,
    source_block,
    target_block,
    block_count,
    tracers,
    east_velocity,
    north_velocity,
    land_mask,
    coupling,
):
    field_count, cell_count = atm_fluxes.shape
    block_cells = remap_weights.shape[-1]
    tile_count = block_count.shape[1]
    slot_count = source_block.shape[1] // tile_count
    tracer_count, level_count, lat_rows, lon_cols = tracers.shape

    atm_blocks = atm_fluxes.reshape(field_count, cell_count // block_cells, block_cells)
    chosen = jnp.take(atm_blocks, source_block[0], axis=1)
    partials = jnp.einsum(
        "fsb,sbc->sfc", chosen, remap_weights[0], preferred_element_type=jnp.float32
    )
    slot_ids = jnp.arange(tile_count * slot_count, dtype=jnp.int32)
    is_live = slot_ids % slot_count < jnp.repeat(block_count[0], slot_count)
    partials = jnp.where(is_live[:, None, None], partials, jnp.float32(0.0))
    targets = jnp.where(is_live, target_block[0], -1).astype(jnp.float32)
    sent = partials.reshape(tile_count, slot_count * field_count, block_cells)
    arrived = lax.all_to_all(sent, ("lat", "lon"), split_axis=0, concat_axis=0, tiled=True)
    landed = lax.all_to_all(
        targets.reshape(tile_count, slot_count),
        ("lat", "lon"),
        split_axis=0,
        concat_axis=0,
        tiled=True,
    )

    sea_here = land_mask.astype(jnp.float32)
    planes = tracer_count * level_count
    stacked = jnp.concatenate(
        [
            tracers.reshape(planes, lat_rows, lon_cols),
            east_velocity,
            north_velocity,
            sea_here[None],
        ],
        axis=0,
    )
    wide = with_halo(stacked, NSUB)
    tracer_now = wide[:planes].reshape(tracer_count, level_count, lat_rows + 2 * NSUB, lon_cols + 2 * NSUB)
    east_wide = wide[planes : planes + level_count]
    north_wide = wide[planes + level_count : planes + 2 * level_count]
    mask_wide = wide[-1]
    for substep in range(NSUB):
        cut = substep
        end_r = lat_rows + 2 * NSUB - cut
        end_c = lon_cols + 2 * NSUB - cut
        tracer_now = advect(
            tracer_now,
            east_wide[:, cut:end_r, cut:end_c],
            north_wide[:, cut:end_r, cut:end_c],
            mask_wide[cut:end_r, cut:end_c],
        )

    arrived = arrived.reshape(tile_count * slot_count, field_count, block_cells)
    landed = landed.reshape(tile_count * slot_count)
    chooser = (landed[None, :] == jnp.arange(lat_rows, dtype=jnp.float32)[:, None]).astype(
        jnp.float32
    )
    ocean_flux = jnp.einsum(
        "rk,kfc->rfc", chooser, arrived, precision=lax.Precision.HIGHEST,
        preferred_element_type=jnp.float32,
    )
    source = jnp.einsum(
        "pf,ifj->pij", coupling, ocean_flux, precision=lax.Precision.HIGHEST
    ).reshape(tracer_count, level_count, lat_rows, lon_cols)
    return tracer_now + sea_here * source


def solution(mesh):
    placed = (
        P(None, ("lat", "lon")),
        P(("lat", "lon"), None, None, None),
        P(("lat", "lon"), None),
        P(("lat", "lon"), None),
        P(("lat", "lon"), None),
        P(None, None, "lat", "lon"),
        P(None, "lat", "lon"),
        P(None, "lat", "lon"),
        P("lat", "lon"),
        P(),
    )
    return jax.shard_map(
        coupled_step,
        mesh=mesh,
        in_specs=placed,
        out_specs=P(None, None, "lat", "lon"),
        check_vma=False,
    )
```

```python
import jax
import jax.numpy as jnp
from jax import lax
from jax.sharding import PartitionSpec as P


NSUB = 4


diffusion_number = 0.2


def shifted_pairs(count, step, wrap):
    pairs = []
    for i in range(count):
        j = i + step
        if 0 <= j < count:
            pairs.append((i, j))
        elif wrap:
            pairs.append((i, j % count))
    return pairs


def with_halo(block, width):
    lon_count = lax.axis_size("lon")
    lat_count = lax.axis_size("lat")
    west = lax.ppermute(block[..., -width:], "lon", shifted_pairs(lon_count, 1, True))
    east = lax.ppermute(block[..., :width], "lon", shifted_pairs(lon_count, -1, True))
    block = jnp.concatenate([west, block, east], axis=-1)
    south = lax.ppermute(block[..., -width:, :], "lat", shifted_pairs(lat_count, 1, False))
    north = lax.ppermute(block[..., :width, :], "lat", shifted_pairs(lat_count, -1, False))
    return jnp.concatenate([south, block, north], axis=-2)


def advect(tracer_now, east_speed, north_speed, sea_mask):
    mask_east = sea_mask[:, :-1] * sea_mask[:, 1:]
    east_flow = mask_east * (
        east_speed[:, :, :-1] * (tracer_now[..., :-1] + tracer_now[..., 1:]) * 0.5
        - diffusion_number * (tracer_now[..., 1:] - tracer_now[..., :-1])
    )
    mask_north = sea_mask[:-1, :] * sea_mask[1:, :]
    north_flow = mask_north * (
        north_speed[:, :-1, :] * (tracer_now[..., :-1, :] + tracer_now[..., 1:, :]) * 0.5
        - diffusion_number * (tracer_now[..., 1:, :] - tracer_now[..., :-1, :])
    )
    inner = tracer_now[..., 1:-1, 1:-1]
    return (
        inner
        + east_flow[..., 1:-1, :-1]
        - east_flow[..., 1:-1, 1:]
        + north_flow[..., :-1, 1:-1]
        - north_flow[..., 1:, 1:-1]
    )


def coupled_step(
    atm_fluxes,
    remap_weights,
    source_block,
    target_block,
    block_count,
    tracers,
    east_velocity,
    north_velocity,
    land_mask,
    coupling,
):
    field_count, cell_count = atm_fluxes.shape
    block_cells = remap_weights.shape[-1]
    tile_count = block_count.shape[1]
    slot_count = source_block.shape[1] // tile_count
    tracer_count, level_count, lat_rows, lon_cols = tracers.shape

    atm_blocks = atm_fluxes.reshape(field_count, cell_count // block_cells, block_cells)
    chosen = jnp.take(atm_blocks, source_block[0], axis=1)
    partials = jnp.einsum(
        "fsb,sbc->sfc", chosen, remap_weights[0], preferred_element_type=jnp.float32
    )
    slot_ids = jnp.arange(tile_count * slot_count, dtype=jnp.int32)
    is_live = slot_ids % slot_count < jnp.repeat(block_count[0], slot_count)
    partials = jnp.where(is_live[:, None, None], partials, jnp.float32(0.0))
    targets = jnp.where(is_live, target_block[0], -1).astype(jnp.float32)
    rows_part = jnp.broadcast_to(
        targets.reshape(tile_count, slot_count, 1), (tile_count, slot_count, block_cells)
    )
    pad_rows = jnp.zeros((tile_count, 8 - slot_count, block_cells), jnp.float32)
    sent = jnp.concatenate(
        [
            partials.reshape(tile_count, slot_count * field_count, block_cells),
            rows_part,
            pad_rows,
        ],
        axis=1,
    )
    arrived = lax.all_to_all(sent, ("lat", "lon"), split_axis=0, concat_axis=0, tiled=True)
    landed = arrived[:, slot_count * field_count : slot_count * (field_count + 1), 0]
    arrived = arrived[:, : slot_count * field_count]

    sea_here = land_mask.astype(jnp.float32)
    planes = tracer_count * level_count
    stacked = jnp.concatenate(
        [
            tracers.reshape(planes, lat_rows, lon_cols),
            east_velocity,
            north_velocity,
            sea_here[None],
        ],
        axis=0,
    )
    wide = with_halo(stacked, NSUB)
    tracer_now = wide[:planes].reshape(tracer_count, level_count, lat_rows + 2 * NSUB, lon_cols + 2 * NSUB)
    east_wide = wide[planes : planes + level_count]
    north_wide = wide[planes + level_count : planes + 2 * level_count]
    mask_wide = wide[-1]
    for substep in range(NSUB):
        cut = substep
        end_r = lat_rows + 2 * NSUB - cut
        end_c = lon_cols + 2 * NSUB - cut
        tracer_now = advect(
            tracer_now,
            east_wide[:, cut:end_r, cut:end_c],
            north_wide[:, cut:end_r, cut:end_c],
            mask_wide[cut:end_r, cut:end_c],
        )

    arrived = arrived.reshape(tile_count * slot_count, field_count, block_cells)
    landed = landed.reshape(tile_count * slot_count)
    chooser = (landed[None, :] == jnp.arange(lat_rows, dtype=jnp.float32)[:, None]).astype(
        jnp.float32
    )
    ocean_flux = jnp.einsum(
        "rk,kfc->rfc", chooser, arrived, precision=lax.Precision.HIGHEST,
        preferred_element_type=jnp.float32,
    )
    source = jnp.einsum(
        "pf,ifj->pij", coupling, ocean_flux, precision=lax.Precision.HIGHEST
    ).reshape(tracer_count, level_count, lat_rows, lon_cols)
    return tracer_now + sea_here * source


def solution(mesh):
    placed = (
        P(None, ("lat", "lon")),
        P(("lat", "lon"), None, None, None),
        P(("lat", "lon"), None),
        P(("lat", "lon"), None),
        P(("lat", "lon"), None),
        P(None, None, "lat", "lon"),
        P(None, "lat", "lon"),
        P(None, "lat", "lon"),
        P("lat", "lon"),
        P(),
    )
    return jax.shard_map(
        coupled_step,
        mesh=mesh,
        in_specs=placed,
        out_specs=P(None, None, "lat", "lon"),
        check_vma=False,
    )
```

```python
import jax
import jax.numpy as jnp
from jax import lax
from jax.experimental import pallas as pl
from jax.experimental.pallas import tpu as pltpu
from jax.sharding import PartitionSpec as P


NSUB = 4


diffusion_number = 0.2


def shifted_pairs(count, step, wrap):
    pairs = []
    for i in range(count):
        j = i + step
        if 0 <= j < count:
            pairs.append((i, j))
        elif wrap:
            pairs.append((i, j % count))
    return pairs


def with_halo(block, width):
    lon_count = lax.axis_size("lon")
    lat_count = lax.axis_size("lat")
    west = lax.ppermute(block[..., -width:], "lon", shifted_pairs(lon_count, 1, True))
    east = lax.ppermute(block[..., :width], "lon", shifted_pairs(lon_count, -1, True))
    block = jnp.concatenate([west, block, east], axis=-1)
    south = lax.ppermute(block[..., -width:, :], "lat", shifted_pairs(lat_count, 1, False))
    north = lax.ppermute(block[..., :width, :], "lat", shifted_pairs(lat_count, -1, False))
    return jnp.concatenate([south, block, north], axis=-2)


TILES_PER_STEP = 16


def remap_kernel(src_ref, tgt_ref, atm_ref, w_ref, out_ref):
    step = pl.program_id(0)
    tiles, _, cells = out_ref.shape
    slots = w_ref.shape[0] // tiles
    fields = atm_ref.shape[1]
    blocks = atm_ref.shape[0]
    row_ids = lax.broadcasted_iota(jnp.int32, (8, cells), 0)

    def one_tile(i, carry):
        tail = jnp.zeros((8, cells), jnp.float32)
        for k in range(slots):
            s = (step * tiles + i) * slots + k
            src = jnp.clip(src_ref[s], 0, blocks - 1)
            tgt = tgt_ref[s]
            part = jnp.dot(atm_ref[src], w_ref[i * slots + k], preferred_element_type=jnp.float32)
            out_ref[i, k * fields : (k + 1) * fields, :] = jnp.where(tgt >= 0, part, jnp.float32(0.0))
            tail = jnp.where(row_ids == k, tgt.astype(jnp.float32), tail)
        out_ref[i, slots * fields : slots * fields + 8, :] = tail
        return carry

    lax.fori_loop(0, tiles, one_tile, 0)


def remap_partials(atm_blocks, weights, sources, targets):
    blocks, fields, cells = atm_blocks.shape
    slot_total = weights.shape[0]
    slots = 2
    tile_count = slot_total // slots
    rows = slots * fields + 8
    per = TILES_PER_STEP
    return pl.pallas_call(
        remap_kernel,
        out_shape=jax.ShapeDtypeStruct((tile_count, rows, cells), jnp.float32),
        grid_spec=pltpu.PrefetchScalarGridSpec(
            num_scalar_prefetch=2,
            grid=(tile_count // per,),
            in_specs=[
                pl.BlockSpec((blocks, fields, cells), lambda g, src, tgt: (0, 0, 0)),
                pl.BlockSpec((per * slots, cells, cells), lambda g, src, tgt: (g, 0, 0)),
            ],
            out_specs=pl.BlockSpec((per, rows, cells), lambda g, src, tgt: (g, 0, 0)),
        ),
        cost_estimate=pl.CostEstimate(
            flops=2 * slot_total * fields * cells * cells,
            transcendentals=0,
            bytes_accessed=slot_total * cells * cells * 2 + tile_count * rows * cells * 4,
        ),
    )(sources, targets, atm_blocks, weights)


def advect(tracer_now, east_speed, north_speed, sea_mask):
    mask_east = sea_mask[:, :-1] * sea_mask[:, 1:]
    east_flow = mask_east * (
        east_speed[:, :, :-1] * (tracer_now[..., :-1] + tracer_now[..., 1:]) * 0.5
        - diffusion_number * (tracer_now[..., 1:] - tracer_now[..., :-1])
    )
    mask_north = sea_mask[:-1, :] * sea_mask[1:, :]
    north_flow = mask_north * (
        north_speed[:, :-1, :] * (tracer_now[..., :-1, :] + tracer_now[..., 1:, :]) * 0.5
        - diffusion_number * (tracer_now[..., 1:, :] - tracer_now[..., :-1, :])
    )
    inner = tracer_now[..., 1:-1, 1:-1]
    return (
        inner
        + east_flow[..., 1:-1, :-1]
        - east_flow[..., 1:-1, 1:]
        + north_flow[..., :-1, 1:-1]
        - north_flow[..., 1:, 1:-1]
    )


def coupled_step(
    atm_fluxes,
    remap_weights,
    source_block,
    target_block,
    block_count,
    tracers,
    east_velocity,
    north_velocity,
    land_mask,
    coupling,
):
    field_count, cell_count = atm_fluxes.shape
    block_cells = remap_weights.shape[-1]
    tile_count = block_count.shape[1]
    slot_count = source_block.shape[1] // tile_count
    tracer_count, level_count, lat_rows, lon_cols = tracers.shape

    slot_ids = jnp.arange(tile_count * slot_count, dtype=jnp.int32)
    is_live = slot_ids % slot_count < jnp.repeat(block_count[0], slot_count)
    targets = jnp.where(is_live, target_block[0], -1)
    atm_blocks = atm_fluxes.reshape(field_count, cell_count // block_cells, block_cells)
    sent = remap_partials(atm_blocks.transpose(1, 0, 2), remap_weights[0], source_block[0], targets)
    arrived = lax.all_to_all(sent, ("lat", "lon"), split_axis=0, concat_axis=0, tiled=True)
    landed = arrived[:, slot_count * field_count : slot_count * (field_count + 1), 0]
    assert slot_count == 2
    arrived = arrived[:, : slot_count * field_count]

    sea_here = land_mask.astype(jnp.float32)
    planes = tracer_count * level_count
    stacked = jnp.concatenate(
        [
            tracers.reshape(planes, lat_rows, lon_cols),
            east_velocity,
            north_velocity,
            sea_here[None],
        ],
        axis=0,
    )
    wide = with_halo(stacked, NSUB)
    tracer_now = wide[:planes].reshape(tracer_count, level_count, lat_rows + 2 * NSUB, lon_cols + 2 * NSUB)
    east_wide = wide[planes : planes + level_count]
    north_wide = wide[planes + level_count : planes + 2 * level_count]
    mask_wide = wide[-1]
    for substep in range(NSUB):
        cut = substep
        end_r = lat_rows + 2 * NSUB - cut
        end_c = lon_cols + 2 * NSUB - cut
        tracer_now = advect(
            tracer_now,
            east_wide[:, cut:end_r, cut:end_c],
            north_wide[:, cut:end_r, cut:end_c],
            mask_wide[cut:end_r, cut:end_c],
        )

    arrived = arrived.reshape(tile_count * slot_count, field_count, block_cells)
    landed = landed.reshape(tile_count * slot_count)
    chooser = (landed[None, :] == jnp.arange(lat_rows, dtype=jnp.float32)[:, None]).astype(
        jnp.float32
    )
    ocean_flux = jnp.einsum(
        "rk,kfc->rfc", chooser, arrived, precision=lax.Precision.HIGHEST,
        preferred_element_type=jnp.float32,
    )
    source = jnp.einsum(
        "pf,ifj->pij", coupling, ocean_flux, precision=lax.Precision.HIGHEST
    ).reshape(tracer_count, level_count, lat_rows, lon_cols)
    return tracer_now + sea_here * source


def solution(mesh):
    placed = (
        P(None, ("lat", "lon")),
        P(("lat", "lon"), None, None, None),
        P(("lat", "lon"), None),
        P(("lat", "lon"), None),
        P(("lat", "lon"), None),
        P(None, None, "lat", "lon"),
        P(None, "lat", "lon"),
        P(None, "lat", "lon"),
        P("lat", "lon"),
        P(),
    )
    return jax.shard_map(
        coupled_step,
        mesh=mesh,
        in_specs=placed,
        out_specs=P(None, None, "lat", "lon"),
        check_vma=False,
    )
```

```python
import jax
import jax.numpy as jnp
from jax import lax
from jax.sharding import PartitionSpec as P


NSUB = 4


diffusion_number = 0.2


def shifted_pairs(count, step, wrap):
    pairs = []
    for i in range(count):
        j = i + step
        if 0 <= j < count:
            pairs.append((i, j))
        elif wrap:
            pairs.append((i, j % count))
    return pairs


def with_halo(block, width):
    lon_count = lax.axis_size("lon")
    lat_count = lax.axis_size("lat")
    planes, rows, cols = block.shape
    west = lax.ppermute(
        block[..., -width:].reshape(planes, rows * width), "lon", shifted_pairs(lon_count, 1, True)
    )
    east = lax.ppermute(
        block[..., :width].reshape(planes, rows * width), "lon", shifted_pairs(lon_count, -1, True)
    )
    west = west.reshape(planes, rows, width)
    east = east.reshape(planes, rows, width)
    middle = jnp.concatenate([west, block, east], axis=-1)
    wide_cols = cols + 2 * width
    south = lax.ppermute(
        middle[:, -width:, :].reshape(planes, width * wide_cols),
        "lat",
        shifted_pairs(lat_count, 1, False),
    )
    north = lax.ppermute(
        middle[:, :width, :].reshape(planes, width * wide_cols),
        "lat",
        shifted_pairs(lat_count, -1, False),
    )
    south = south.reshape(planes, width, wide_cols)
    north = north.reshape(planes, width, wide_cols)
    return jnp.concatenate([south, middle, north], axis=-2)


def advect(tracer_now, east_speed, north_speed, sea_mask):
    mask_east = sea_mask[:, :-1] * sea_mask[:, 1:]
    east_flow = mask_east * (
        east_speed[:, :, :-1] * (tracer_now[..., :-1] + tracer_now[..., 1:]) * 0.5
        - diffusion_number * (tracer_now[..., 1:] - tracer_now[..., :-1])
    )
    mask_north = sea_mask[:-1, :] * sea_mask[1:, :]
    north_flow = mask_north * (
        north_speed[:, :-1, :] * (tracer_now[..., :-1, :] + tracer_now[..., 1:, :]) * 0.5
        - diffusion_number * (tracer_now[..., 1:, :] - tracer_now[..., :-1, :])
    )
    inner = tracer_now[..., 1:-1, 1:-1]
    return (
        inner
        + east_flow[..., 1:-1, :-1]
        - east_flow[..., 1:-1, 1:]
        + north_flow[..., :-1, 1:-1]
        - north_flow[..., 1:, 1:-1]
    )


def coupled_step(
    atm_fluxes,
    remap_weights,
    source_block,
    target_block,
    block_count,
    tracers,
    east_velocity,
    north_velocity,
    land_mask,
    coupling,
):
    field_count, cell_count = atm_fluxes.shape
    block_cells = remap_weights.shape[-1]
    tile_count = block_count.shape[1]
    slot_count = source_block.shape[1] // tile_count
    tracer_count, level_count, lat_rows, lon_cols = tracers.shape

    atm_blocks = atm_fluxes.reshape(field_count, cell_count // block_cells, block_cells)
    chosen = jnp.take(atm_blocks, source_block[0], axis=1)
    partials = jnp.einsum(
        "fsb,sbc->sfc", chosen, remap_weights[0], preferred_element_type=jnp.float32
    )
    slot_ids = jnp.arange(tile_count * slot_count, dtype=jnp.int32)
    is_live = slot_ids % slot_count < jnp.repeat(block_count[0], slot_count)
    partials = jnp.where(is_live[:, None, None], partials, jnp.float32(0.0))
    targets = jnp.where(is_live, target_block[0], -1).astype(jnp.float32)
    rows_part = jnp.broadcast_to(
        targets.reshape(tile_count, slot_count, 1), (tile_count, slot_count, block_cells)
    )
    pad_rows = jnp.zeros((tile_count, 8 - slot_count, block_cells), jnp.float32)
    sent = jnp.concatenate(
        [
            partials.reshape(tile_count, slot_count * field_count, block_cells),
            rows_part,
            pad_rows,
        ],
        axis=1,
    )
    arrived = lax.all_to_all(sent, ("lat", "lon"), split_axis=0, concat_axis=0, tiled=True)
    landed = arrived[:, slot_count * field_count : slot_count * (field_count + 1), 0]
    arrived = arrived[:, : slot_count * field_count]

    sea_here = land_mask.astype(jnp.float32)
    planes = tracer_count * level_count
    stacked = jnp.concatenate(
        [
            tracers.reshape(planes, lat_rows, lon_cols),
            east_velocity,
            north_velocity,
            sea_here[None],
        ],
        axis=0,
    )
    wide = with_halo(stacked, NSUB)
    tracer_now = wide[:planes].reshape(tracer_count, level_count, lat_rows + 2 * NSUB, lon_cols + 2 * NSUB)
    east_wide = wide[planes : planes + level_count]
    north_wide = wide[planes + level_count : planes + 2 * level_count]
    mask_wide = wide[-1]
    for substep in range(NSUB):
        cut = substep
        end_r = lat_rows + 2 * NSUB - cut
        end_c = lon_cols + 2 * NSUB - cut
        tracer_now = advect(
            tracer_now,
            east_wide[:, cut:end_r, cut:end_c],
            north_wide[:, cut:end_r, cut:end_c],
            mask_wide[cut:end_r, cut:end_c],
        )

    arrived = arrived.reshape(tile_count * slot_count, field_count, block_cells)
    landed = landed.reshape(tile_count * slot_count)
    chooser = (landed[None, :] == jnp.arange(lat_rows, dtype=jnp.float32)[:, None]).astype(
        jnp.float32
    )
    ocean_flux = jnp.einsum(
        "rk,kfc->rfc", chooser, arrived, precision=lax.Precision.HIGHEST,
        preferred_element_type=jnp.float32,
    )
    source = jnp.einsum(
        "pf,ifj->pij", coupling, ocean_flux, precision=lax.Precision.HIGHEST
    ).reshape(tracer_count, level_count, lat_rows, lon_cols)
    return tracer_now + sea_here * source


def solution(mesh):
    placed = (
        P(None, ("lat", "lon")),
        P(("lat", "lon"), None, None, None),
        P(("lat", "lon"), None),
        P(("lat", "lon"), None),
        P(("lat", "lon"), None),
        P(None, None, "lat", "lon"),
        P(None, "lat", "lon"),
        P(None, "lat", "lon"),
        P("lat", "lon"),
        P(),
    )
    return jax.shard_map(
        coupled_step,
        mesh=mesh,
        in_specs=placed,
        out_specs=P(None, None, "lat", "lon"),
        check_vma=False,
    )
```

```python
import jax
import jax.numpy as jnp
from jax import lax
from jax.sharding import PartitionSpec as P


NSUB = 4


diffusion_number = 0.2


def shifted_pairs(count, step, wrap):
    pairs = []
    for i in range(count):
        j = i + step
        if 0 <= j < count:
            pairs.append((i, j))
        elif wrap:
            pairs.append((i, j % count))
    return pairs


def with_halo(block, width):
    lon_count = lax.axis_size("lon")
    lat_count = lax.axis_size("lat")
    planes, rows, cols = block.shape
    west = lax.ppermute(
        block[..., -width:].reshape(planes, rows * width), "lon", shifted_pairs(lon_count, 1, True)
    )
    east = lax.ppermute(
        block[..., :width].reshape(planes, rows * width), "lon", shifted_pairs(lon_count, -1, True)
    )
    west = west.reshape(planes, rows, width)
    east = east.reshape(planes, rows, width)
    middle = jnp.concatenate([west, block, east], axis=-1)
    wide_cols = cols + 2 * width
    south = lax.ppermute(
        middle[:, -width:, :].reshape(planes, width * wide_cols),
        "lat",
        shifted_pairs(lat_count, 1, False),
    )
    north = lax.ppermute(
        middle[:, :width, :].reshape(planes, width * wide_cols),
        "lat",
        shifted_pairs(lat_count, -1, False),
    )
    south = south.reshape(planes, width, wide_cols)
    north = north.reshape(planes, width, wide_cols)
    return jnp.concatenate([south, middle, north], axis=-2)


def advect(tracer_now, east_speed, north_speed, sea_mask):
    mask_east = sea_mask[:, :-1] * sea_mask[:, 1:]
    east_flow = mask_east * (
        east_speed[:, :, :-1] * (tracer_now[..., :-1] + tracer_now[..., 1:]) * 0.5
        - diffusion_number * (tracer_now[..., 1:] - tracer_now[..., :-1])
    )
    mask_north = sea_mask[:-1, :] * sea_mask[1:, :]
    north_flow = mask_north * (
        north_speed[:, :-1, :] * (tracer_now[..., :-1, :] + tracer_now[..., 1:, :]) * 0.5
        - diffusion_number * (tracer_now[..., 1:, :] - tracer_now[..., :-1, :])
    )
    inner = tracer_now[..., 1:-1, 1:-1]
    return (
        inner
        + east_flow[..., 1:-1, :-1]
        - east_flow[..., 1:-1, 1:]
        + north_flow[..., :-1, 1:-1]
        - north_flow[..., 1:, 1:-1]
    )


def coupled_step(
    atm_fluxes,
    remap_weights,
    source_block,
    target_block,
    block_count,
    tracers,
    east_velocity,
    north_velocity,
    land_mask,
    coupling,
):
    field_count, cell_count = atm_fluxes.shape
    block_cells = remap_weights.shape[-1]
    tile_count = block_count.shape[1]
    slot_count = source_block.shape[1] // tile_count
    tracer_count, level_count, lat_rows, lon_cols = tracers.shape

    slot_ids = jnp.arange(tile_count * slot_count, dtype=jnp.int32)
    is_live = slot_ids % slot_count < jnp.repeat(block_count[0], slot_count)
    targets = jnp.where(is_live, target_block[0], -1).astype(jnp.float32)
    atm_blocks = atm_fluxes.reshape(field_count, cell_count // block_cells, block_cells)
    chosen = jnp.take(atm_blocks, source_block[0], axis=1)
    chosen = chosen.transpose(1, 0, 2).reshape(tile_count, slot_count, field_count, block_cells)
    zero_block = jnp.zeros((tile_count, field_count, block_cells), chosen.dtype)
    diagonal = []
    for k in range(slot_count):
        diagonal.append(
            jnp.concatenate(
                [chosen[:, k] if j == k else zero_block for j in range(slot_count)], axis=-1
            )
        )
    diagonal.append(jnp.zeros((tile_count, 8, slot_count * block_cells), chosen.dtype))
    lhs = jnp.concatenate(diagonal, axis=1)
    stacked_weights = remap_weights[0].reshape(tile_count, slot_count * block_cells, block_cells)
    product = jnp.einsum(
        "trb,tbc->trc", lhs, stacked_weights, preferred_element_type=jnp.float32
    )
    row_ids = jnp.arange(slot_count * field_count + 8)
    slot_of_row = row_ids // field_count
    live_rows = is_live.reshape(tile_count, slot_count)
    tgt_rows = targets.reshape(tile_count, slot_count)
    kept = jnp.zeros((tile_count, slot_count * field_count + 8), jnp.bool_)
    tail = jnp.zeros((tile_count, slot_count * field_count + 8), jnp.float32)
    for k in range(slot_count):
        kept = kept | ((slot_of_row == k)[None, :] & live_rows[:, k : k + 1])
        tail = jnp.where(
            (row_ids == slot_count * field_count + k)[None, :], tgt_rows[:, k : k + 1], tail
        )
    sent = jnp.where(
        (row_ids < slot_count * field_count)[None, :, None],
        jnp.where(kept[:, :, None], product, jnp.float32(0.0)),
        tail[:, :, None],
    )
    arrived = lax.all_to_all(sent, ("lat", "lon"), split_axis=0, concat_axis=0, tiled=True)
    landed = arrived[:, slot_count * field_count : slot_count * (field_count + 1), 0]
    arrived = arrived[:, : slot_count * field_count]

    sea_here = land_mask.astype(jnp.float32)
    planes = tracer_count * level_count
    stacked = jnp.concatenate(
        [
            tracers.reshape(planes, lat_rows, lon_cols),
            east_velocity,
            north_velocity,
            sea_here[None],
        ],
        axis=0,
    )
    wide = with_halo(stacked, NSUB)
    tracer_now = wide[:planes].reshape(tracer_count, level_count, lat_rows + 2 * NSUB, lon_cols + 2 * NSUB)
    east_wide = wide[planes : planes + level_count]
    north_wide = wide[planes + level_count : planes + 2 * level_count]
    mask_wide = wide[-1]
    for substep in range(NSUB):
        cut = substep
        end_r = lat_rows + 2 * NSUB - cut
        end_c = lon_cols + 2 * NSUB - cut
        tracer_now = advect(
            tracer_now,
            east_wide[:, cut:end_r, cut:end_c],
            north_wide[:, cut:end_r, cut:end_c],
            mask_wide[cut:end_r, cut:end_c],
        )

    arrived = arrived.reshape(tile_count * slot_count, field_count, block_cells)
    landed = landed.reshape(tile_count * slot_count)
    chooser = (landed[None, :] == jnp.arange(lat_rows, dtype=jnp.float32)[:, None]).astype(
        jnp.float32
    )
    ocean_flux = jnp.einsum(
        "rk,kfc->rfc", chooser, arrived, precision=lax.Precision.HIGHEST,
        preferred_element_type=jnp.float32,
    )
    source = jnp.einsum(
        "pf,ifj->pij", coupling, ocean_flux, precision=lax.Precision.HIGHEST
    ).reshape(tracer_count, level_count, lat_rows, lon_cols)
    return tracer_now + sea_here * source


def solution(mesh):
    placed = (
        P(None, ("lat", "lon")),
        P(("lat", "lon"), None, None, None),
        P(("lat", "lon"), None),
        P(("lat", "lon"), None),
        P(("lat", "lon"), None),
        P(None, None, "lat", "lon"),
        P(None, "lat", "lon"),
        P(None, "lat", "lon"),
        P("lat", "lon"),
        P(),
    )
    return jax.shard_map(
        coupled_step,
        mesh=mesh,
        in_specs=placed,
        out_specs=P(None, None, "lat", "lon"),
        check_vma=False,
    )
```

```python
import jax
import jax.numpy as jnp
from jax import lax
from jax.sharding import PartitionSpec as P


NSUB = 4


diffusion_number = 0.2


def shifted_pairs(count, step, wrap):
    pairs = []
    for i in range(count):
        j = i + step
        if 0 <= j < count:
            pairs.append((i, j))
        elif wrap:
            pairs.append((i, j % count))
    return pairs


def with_halo(block, width):
    lon_count = lax.axis_size("lon")
    lat_count = lax.axis_size("lat")
    planes, rows, cols = block.shape
    west = lax.ppermute(
        block[..., -width:].reshape(planes, rows * width), "lon", shifted_pairs(lon_count, 1, True)
    )
    east = lax.ppermute(
        block[..., :width].reshape(planes, rows * width), "lon", shifted_pairs(lon_count, -1, True)
    )
    west = west.reshape(planes, rows, width)
    east = east.reshape(planes, rows, width)
    middle = jnp.concatenate([west, block, east], axis=-1)
    wide_cols = cols + 2 * width
    south = lax.ppermute(
        middle[:, -width:, :].reshape(planes, width * wide_cols),
        "lat",
        shifted_pairs(lat_count, 1, False),
    )
    north = lax.ppermute(
        middle[:, :width, :].reshape(planes, width * wide_cols),
        "lat",
        shifted_pairs(lat_count, -1, False),
    )
    south = south.reshape(planes, width, wide_cols)
    north = north.reshape(planes, width, wide_cols)
    return jnp.concatenate([south, middle, north], axis=-2)


def advect(tracer_now, east_speed, north_speed, sea_mask):
    mask_east = sea_mask[:, :-1] * sea_mask[:, 1:]
    east_flow = mask_east * (
        east_speed[:, :, :-1] * (tracer_now[..., :-1] + tracer_now[..., 1:]) * 0.5
        - diffusion_number * (tracer_now[..., 1:] - tracer_now[..., :-1])
    )
    mask_north = sea_mask[:-1, :] * sea_mask[1:, :]
    north_flow = mask_north * (
        north_speed[:, :-1, :] * (tracer_now[..., :-1, :] + tracer_now[..., 1:, :]) * 0.5
        - diffusion_number * (tracer_now[..., 1:, :] - tracer_now[..., :-1, :])
    )
    inner = tracer_now[..., 1:-1, 1:-1]
    return (
        inner
        + east_flow[..., 1:-1, :-1]
        - east_flow[..., 1:-1, 1:]
        + north_flow[..., :-1, 1:-1]
        - north_flow[..., 1:, 1:-1]
    )


def coupled_step(
    atm_fluxes,
    remap_weights,
    source_block,
    target_block,
    block_count,
    tracers,
    east_velocity,
    north_velocity,
    land_mask,
    coupling,
):
    field_count, cell_count = atm_fluxes.shape
    block_cells = remap_weights.shape[-1]
    tile_count = block_count.shape[1]
    slot_count = source_block.shape[1] // tile_count
    tracer_count, level_count, lat_rows, lon_cols = tracers.shape

    slot_ids = jnp.arange(tile_count * slot_count, dtype=jnp.int32)
    is_live = slot_ids % slot_count < jnp.repeat(block_count[0], slot_count)
    targets = jnp.where(is_live, target_block[0], -1).astype(jnp.float32)
    atm_blocks = atm_fluxes.reshape(field_count, cell_count // block_cells, block_cells)
    chosen = jnp.take(atm_blocks, source_block[0], axis=1)
    chosen = chosen.transpose(1, 0, 2).reshape(tile_count, slot_count, field_count, block_cells)
    zero_block = jnp.zeros((tile_count, field_count, block_cells), chosen.dtype)
    diagonal = []
    for k in range(slot_count):
        diagonal.append(
            jnp.concatenate(
                [chosen[:, k] if j == k else zero_block for j in range(slot_count)], axis=-1
            )
        )
    diagonal.append(jnp.zeros((tile_count, 8, slot_count * block_cells), chosen.dtype))
    lhs = jnp.concatenate(diagonal, axis=1)
    stacked_weights = remap_weights[0].reshape(tile_count, slot_count * block_cells, block_cells)
    product = jnp.einsum("trb,tbc->trc", lhs, stacked_weights, preferred_element_type=jnp.float32)
    row_ids = jnp.arange(slot_count * field_count + 8)
    slot_of_row = row_ids // field_count
    live_rows = is_live.reshape(tile_count, slot_count)
    tgt_rows = targets.reshape(tile_count, slot_count)
    kept = jnp.zeros((tile_count, slot_count * field_count + 8), jnp.bool_)
    tail = jnp.zeros((tile_count, slot_count * field_count + 8), jnp.float32)
    for k in range(slot_count):
        kept = kept | ((slot_of_row == k)[None, :] & live_rows[:, k : k + 1])
        tail = jnp.where(
            (row_ids == slot_count * field_count + k)[None, :], tgt_rows[:, k : k + 1], tail
        )
    sent = jnp.where(
        (row_ids < slot_count * field_count)[None, :, None],
        jnp.where(kept[:, :, None], product, jnp.float32(0.0)),
        tail[:, :, None],
    )
    arrived = lax.all_to_all(sent, ("lat", "lon"), split_axis=0, concat_axis=0, tiled=True)
    arrived_all = arrived
    landed = arrived[:, slot_count * field_count : slot_count * (field_count + 1), 0]

    sea_here = land_mask.astype(jnp.float32)
    planes = tracer_count * level_count
    stacked = jnp.concatenate(
        [
            tracers.reshape(planes, lat_rows, lon_cols),
            east_velocity,
            north_velocity,
            sea_here[None],
        ],
        axis=0,
    )
    wide = with_halo(stacked, NSUB)
    tracer_now = wide[:planes].reshape(tracer_count, level_count, lat_rows + 2 * NSUB, lon_cols + 2 * NSUB)
    east_wide = wide[planes : planes + level_count]
    north_wide = wide[planes + level_count : planes + 2 * level_count]
    mask_wide = wide[-1]
    for substep in range(NSUB):
        cut = substep
        end_r = lat_rows + 2 * NSUB - cut
        end_c = lon_cols + 2 * NSUB - cut
        tracer_now = advect(
            tracer_now,
            east_wide[:, cut:end_r, cut:end_c],
            north_wide[:, cut:end_r, cut:end_c],
            mask_wide[cut:end_r, cut:end_c],
        )

    groups = (slot_count * field_count + 8) // 8
    per_slot = field_count // 8
    chooser = (
        landed[None, :, :] == jnp.arange(lat_rows, dtype=jnp.float32)[:, None, None]
    ).astype(jnp.float32)
    group_ids = jnp.arange(groups)
    placement = (
        group_ids[None, None, :]
        == (jnp.arange(slot_count)[:, None, None] * per_slot + jnp.arange(per_slot)[None, :, None])
    ).astype(jnp.float32)
    picker = jnp.einsum("rtk,kjg->rjtg", chooser, placement)
    ocean_flux = jnp.einsum(
        "rjtg,tgic->rjic",
        picker,
        arrived_all.reshape(tile_count, groups, 8, block_cells),
        precision=lax.Precision.HIGHEST,
        preferred_element_type=jnp.float32,
    ).reshape(lat_rows, field_count, block_cells)
    source = jnp.einsum(
        "pf,ifj->pij", coupling, ocean_flux, precision=lax.Precision.HIGHEST
    ).reshape(tracer_count, level_count, lat_rows, lon_cols)
    return tracer_now + sea_here * source


def solution(mesh):
    placed = (
        P(None, ("lat", "lon")),
        P(("lat", "lon"), None, None, None),
        P(("lat", "lon"), None),
        P(("lat", "lon"), None),
        P(("lat", "lon"), None),
        P(None, None, "lat", "lon"),
        P(None, "lat", "lon"),
        P(None, "lat", "lon"),
        P("lat", "lon"),
        P(),
    )
    return jax.shard_map(
        coupled_step,
        mesh=mesh,
        in_specs=placed,
        out_specs=P(None, None, "lat", "lon"),
        check_vma=False,
    )
```

```python
import jax
import jax.numpy as jnp
from jax import lax
from jax.sharding import PartitionSpec as P


NSUB = 4


diffusion_number = 0.2


def shifted_pairs(count, step, wrap):
    pairs = []
    for i in range(count):
        j = i + step
        if 0 <= j < count:
            pairs.append((i, j))
        elif wrap:
            pairs.append((i, j % count))
    return pairs


def with_halo(parts, width):
    lon_count = lax.axis_size("lon")
    lat_count = lax.axis_size("lat")
    rows, cols = parts[0].shape[-2:]
    planes = sum(p.shape[0] for p in parts)
    east_edge = jnp.concatenate([p[..., -width:] for p in parts], axis=0)
    west_edge = jnp.concatenate([p[..., :width] for p in parts], axis=0)
    west = lax.ppermute(
        east_edge.reshape(planes, rows * width), "lon", shifted_pairs(lon_count, 1, True)
    )
    east = lax.ppermute(
        west_edge.reshape(planes, rows * width), "lon", shifted_pairs(lon_count, -1, True)
    )
    west_flat, east_flat = west, east
    west = west.reshape(planes, rows, width)
    east = east.reshape(planes, rows, width)
    wide_cols = cols + 2 * width
    top_rows = jnp.concatenate([p[:, -width:, :] for p in parts], axis=0)
    bottom_rows = jnp.concatenate([p[:, :width, :] for p in parts], axis=0)
    top = jnp.concatenate(
        [west[:, -width:, :], top_rows, east[:, -width:, :]], axis=-1
    ).reshape(planes, width * wide_cols)
    bottom = jnp.concatenate(
        [west[:, :width, :], bottom_rows, east[:, :width, :]], axis=-1
    ).reshape(planes, width * wide_cols)
    south = lax.ppermute(top, "lat", shifted_pairs(lat_count, 1, False))
    north = lax.ppermute(bottom, "lat", shifted_pairs(lat_count, -1, False))
    middle = jnp.concatenate(
        [
            west_flat.reshape(planes, rows, width),
            jnp.concatenate(parts, axis=0),
            east_flat.reshape(planes, rows, width),
        ],
        axis=-1,
    )
    south = south.reshape(planes, width, wide_cols)
    north = north.reshape(planes, width, wide_cols)
    return jnp.concatenate([south, middle, north], axis=-2)


def advect(tracer_now, east_speed, north_speed, sea_mask):
    mask_east = sea_mask[:, :-1] * sea_mask[:, 1:]
    east_flow = mask_east * (
        east_speed[:, :, :-1] * (tracer_now[..., :-1] + tracer_now[..., 1:]) * 0.5
        - diffusion_number * (tracer_now[..., 1:] - tracer_now[..., :-1])
    )
    mask_north = sea_mask[:-1, :] * sea_mask[1:, :]
    north_flow = mask_north * (
        north_speed[:, :-1, :] * (tracer_now[..., :-1, :] + tracer_now[..., 1:, :]) * 0.5
        - diffusion_number * (tracer_now[..., 1:, :] - tracer_now[..., :-1, :])
    )
    inner = tracer_now[..., 1:-1, 1:-1]
    return (
        inner
        + east_flow[..., 1:-1, :-1]
        - east_flow[..., 1:-1, 1:]
        + north_flow[..., :-1, 1:-1]
        - north_flow[..., 1:, 1:-1]
    )


def coupled_step(
    atm_fluxes,
    remap_weights,
    source_block,
    target_block,
    block_count,
    tracers,
    east_velocity,
    north_velocity,
    land_mask,
    coupling,
):
    field_count, cell_count = atm_fluxes.shape
    block_cells = remap_weights.shape[-1]
    tile_count = block_count.shape[1]
    slot_count = source_block.shape[1] // tile_count
    tracer_count, level_count, lat_rows, lon_cols = tracers.shape

    slot_ids = jnp.arange(tile_count * slot_count, dtype=jnp.int32)
    is_live = slot_ids % slot_count < jnp.repeat(block_count[0], slot_count)
    targets = jnp.where(is_live, target_block[0], -1).astype(jnp.float32)
    atm_blocks = atm_fluxes.reshape(field_count, cell_count // block_cells, block_cells)
    chosen = jnp.take(atm_blocks, source_block[0], axis=1)
    chosen = chosen.transpose(1, 0, 2).reshape(tile_count, slot_count, field_count, block_cells)
    zero_block = jnp.zeros((tile_count, field_count, block_cells), chosen.dtype)
    diagonal = []
    for k in range(slot_count):
        diagonal.append(
            jnp.concatenate(
                [chosen[:, k] if j == k else zero_block for j in range(slot_count)], axis=-1
            )
        )
    diagonal.append(jnp.zeros((tile_count, 8, slot_count * block_cells), chosen.dtype))
    lhs = jnp.concatenate(diagonal, axis=1)
    stacked_weights = remap_weights[0].reshape(tile_count, slot_count * block_cells, block_cells)
    product = jnp.einsum("trb,tbc->trc", lhs, stacked_weights, preferred_element_type=jnp.float32)
    row_ids = jnp.arange(slot_count * field_count + 8)
    slot_of_row = row_ids // field_count
    live_rows = is_live.reshape(tile_count, slot_count)
    tgt_rows = targets.reshape(tile_count, slot_count)
    kept = jnp.zeros((tile_count, slot_count * field_count + 8), jnp.bool_)
    tail = jnp.zeros((tile_count, slot_count * field_count + 8), jnp.float32)
    for k in range(slot_count):
        kept = kept | ((slot_of_row == k)[None, :] & live_rows[:, k : k + 1])
        tail = jnp.where(
            (row_ids == slot_count * field_count + k)[None, :], tgt_rows[:, k : k + 1], tail
        )
    sent = jnp.where(
        (row_ids < slot_count * field_count)[None, :, None],
        jnp.where(kept[:, :, None], product, jnp.float32(0.0)),
        tail[:, :, None],
    )
    arrived = lax.all_to_all(sent, ("lat", "lon"), split_axis=0, concat_axis=0, tiled=True)
    landed = arrived[:, slot_count * field_count : slot_count * (field_count + 1), 0]
    arrived = arrived[:, : slot_count * field_count]

    sea_here = land_mask.astype(jnp.float32)
    planes = tracer_count * level_count
    stacked = [
        tracers.reshape(planes, lat_rows, lon_cols),
        east_velocity,
        north_velocity,
        sea_here[None],
    ]
    wide = with_halo(stacked, NSUB)
    tracer_now = wide[:planes].reshape(tracer_count, level_count, lat_rows + 2 * NSUB, lon_cols + 2 * NSUB)
    east_wide = wide[planes : planes + level_count]
    north_wide = wide[planes + level_count : planes + 2 * level_count]
    mask_wide = wide[-1]
    for substep in range(NSUB):
        cut = substep
        end_r = lat_rows + 2 * NSUB - cut
        end_c = lon_cols + 2 * NSUB - cut
        tracer_now = advect(
            tracer_now,
            east_wide[:, cut:end_r, cut:end_c],
            north_wide[:, cut:end_r, cut:end_c],
            mask_wide[cut:end_r, cut:end_c],
        )

    arrived = arrived.reshape(tile_count * slot_count, field_count, block_cells)
    landed = landed.reshape(tile_count * slot_count)
    chooser = (landed[None, :] == jnp.arange(lat_rows, dtype=jnp.float32)[:, None]).astype(
        jnp.float32
    )
    ocean_flux = jnp.einsum(
        "rk,kfc->rfc", chooser, arrived, precision=lax.Precision.HIGHEST,
        preferred_element_type=jnp.float32,
    )
    source = jnp.einsum(
        "pf,ifj->pij", coupling, ocean_flux, precision=lax.Precision.HIGHEST
    ).reshape(tracer_count, level_count, lat_rows, lon_cols)
    return tracer_now + sea_here * source


def solution(mesh):
    placed = (
        P(None, ("lat", "lon")),
        P(("lat", "lon"), None, None, None),
        P(("lat", "lon"), None),
        P(("lat", "lon"), None),
        P(("lat", "lon"), None),
        P(None, None, "lat", "lon"),
        P(None, "lat", "lon"),
        P(None, "lat", "lon"),
        P("lat", "lon"),
        P(),
    )
    return jax.shard_map(
        coupled_step,
        mesh=mesh,
        in_specs=placed,
        out_specs=P(None, None, "lat", "lon"),
        check_vma=False,
    )
```

```python
import jax
import jax.numpy as jnp
from jax import lax
from jax.sharding import PartitionSpec as P


NSUB = 4


diffusion_number = 0.2


def shifted_pairs(count, step, wrap):
    pairs = []
    for i in range(count):
        j = i + step
        if 0 <= j < count:
            pairs.append((i, j))
        elif wrap:
            pairs.append((i, j % count))
    return pairs


def with_halo(block, width):
    lon_count = lax.axis_size("lon")
    lat_count = lax.axis_size("lat")
    planes, rows, cols = block.shape
    west = lax.ppermute(
        block[..., -width:].reshape(planes, rows * width), "lon", shifted_pairs(lon_count, 1, True)
    )
    east = lax.ppermute(
        block[..., :width].reshape(planes, rows * width), "lon", shifted_pairs(lon_count, -1, True)
    )
    west = west.reshape(planes, rows, width)
    east = east.reshape(planes, rows, width)
    wide_cols = cols + 2 * width
    top = jnp.concatenate(
        [west[:, -width:, :], block[:, -width:, :], east[:, -width:, :]], axis=-1
    ).reshape(planes, width * wide_cols)
    bottom = jnp.concatenate(
        [west[:, :width, :], block[:, :width, :], east[:, :width, :]], axis=-1
    ).reshape(planes, width * wide_cols)
    south = lax.ppermute(top, "lat", shifted_pairs(lat_count, 1, False))
    north = lax.ppermute(bottom, "lat", shifted_pairs(lat_count, -1, False))
    middle = jnp.concatenate([west, block, east], axis=-1)
    south = south.reshape(planes, width, wide_cols)
    north = north.reshape(planes, width, wide_cols)
    return jnp.concatenate([south, middle, north], axis=-2)


def advect(tracer_now, east_speed, north_speed, sea_mask):
    mask_east = sea_mask[:, :-1] * sea_mask[:, 1:]
    east_flow = mask_east * (
        east_speed[:, :, :-1] * (tracer_now[..., :-1] + tracer_now[..., 1:]) * 0.5
        - diffusion_number * (tracer_now[..., 1:] - tracer_now[..., :-1])
    )
    mask_north = sea_mask[:-1, :] * sea_mask[1:, :]
    north_flow = mask_north * (
        north_speed[:, :-1, :] * (tracer_now[..., :-1, :] + tracer_now[..., 1:, :]) * 0.5
        - diffusion_number * (tracer_now[..., 1:, :] - tracer_now[..., :-1, :])
    )
    inner = tracer_now[..., 1:-1, 1:-1]
    return (
        inner
        + east_flow[..., 1:-1, :-1]
        - east_flow[..., 1:-1, 1:]
        + north_flow[..., :-1, 1:-1]
        - north_flow[..., 1:, 1:-1]
    )


def coupled_step(
    atm_fluxes,
    remap_weights,
    source_block,
    target_block,
    block_count,
    tracers,
    east_velocity,
    north_velocity,
    land_mask,
    coupling,
):
    field_count, cell_count = atm_fluxes.shape
    block_cells = remap_weights.shape[-1]
    tile_count = block_count.shape[1]
    slot_count = source_block.shape[1] // tile_count
    tracer_count, level_count, lat_rows, lon_cols = tracers.shape

    slot_ids = jnp.arange(tile_count * slot_count, dtype=jnp.int32)
    is_live = slot_ids % slot_count < jnp.repeat(block_count[0], slot_count)
    targets = jnp.where(is_live, target_block[0], -1).astype(jnp.float32)
    atm_blocks = atm_fluxes.reshape(field_count, cell_count // block_cells, block_cells)
    chosen = jnp.take(atm_blocks, source_block[0], axis=1)
    chosen = chosen.transpose(1, 0, 2).reshape(tile_count, slot_count, field_count, block_cells)
    zero_block = jnp.zeros((tile_count, field_count, block_cells), chosen.dtype)
    diagonal = []
    for k in range(slot_count):
        diagonal.append(
            jnp.concatenate(
                [chosen[:, k] if j == k else zero_block for j in range(slot_count)], axis=-1
            )
        )
    diagonal.append(jnp.zeros((tile_count, 8, slot_count * block_cells), chosen.dtype))
    lhs = jnp.concatenate(diagonal, axis=1)
    stacked_weights = remap_weights[0].reshape(tile_count, slot_count * block_cells, block_cells)
    product = jnp.einsum(
        "trb,tbc->trc", lhs, stacked_weights, preferred_element_type=jnp.float32
    )
    row_ids = jnp.arange(slot_count * field_count + 8)
    slot_of_row = row_ids // field_count
    live_rows = is_live.reshape(tile_count, slot_count)
    tgt_rows = targets.reshape(tile_count, slot_count)
    kept = jnp.zeros((tile_count, slot_count * field_count + 8), jnp.bool_)
    tail = jnp.zeros((tile_count, slot_count * field_count + 8), jnp.float32)
    for k in range(slot_count):
        kept = kept | ((slot_of_row == k)[None, :] & live_rows[:, k : k + 1])
        tail = jnp.where(
            (row_ids == slot_count * field_count + k)[None, :], tgt_rows[:, k : k + 1], tail
        )
    sent = jnp.where(
        (row_ids < slot_count * field_count)[None, :, None],
        jnp.where(kept[:, :, None], product, jnp.float32(0.0)),
        tail[:, :, None],
    )
    arrived = lax.all_to_all(sent, ("lat", "lon"), split_axis=0, concat_axis=0, tiled=True)
    landed = arrived[:, slot_count * field_count : slot_count * (field_count + 1), 0]
    arrived = arrived[:, : slot_count * field_count]

    sea_here = land_mask.astype(jnp.float32)
    planes = tracer_count * level_count
    stacked = jnp.concatenate(
        [
            tracers.reshape(planes, lat_rows, lon_cols),
            east_velocity,
            north_velocity,
            sea_here[None],
        ],
        axis=0,
    )
    wide = with_halo(stacked, NSUB)
    tracer_now = wide[:planes].reshape(tracer_count, level_count, lat_rows + 2 * NSUB, lon_cols + 2 * NSUB)
    east_wide = wide[planes : planes + level_count]
    north_wide = wide[planes + level_count : planes + 2 * level_count]
    mask_wide = wide[-1]
    for substep in range(NSUB):
        cut = substep
        end_r = lat_rows + 2 * NSUB - cut
        end_c = lon_cols + 2 * NSUB - cut
        tracer_now = advect(
            tracer_now,
            east_wide[:, cut:end_r, cut:end_c],
            north_wide[:, cut:end_r, cut:end_c],
            mask_wide[cut:end_r, cut:end_c],
        )

    arrived = arrived.reshape(tile_count * slot_count, field_count, block_cells)
    landed = landed.reshape(tile_count * slot_count)
    chooser = (landed[None, :] == jnp.arange(lat_rows, dtype=jnp.float32)[:, None]).astype(
        jnp.float32
    )
    ocean_flux = jnp.einsum(
        "rk,kfc->rfc", chooser, arrived, precision=lax.Precision.HIGH,
        preferred_element_type=jnp.float32,
    )
    source = jnp.einsum(
        "pf,ifj->pij", coupling, ocean_flux, precision=lax.Precision.HIGH
    ).reshape(tracer_count, level_count, lat_rows, lon_cols)
    return tracer_now + sea_here * source


def solution(mesh):
    placed = (
        P(None, ("lat", "lon")),
        P(("lat", "lon"), None, None, None),
        P(("lat", "lon"), None),
        P(("lat", "lon"), None),
        P(("lat", "lon"), None),
        P(None, None, "lat", "lon"),
        P(None, "lat", "lon"),
        P(None, "lat", "lon"),
        P("lat", "lon"),
        P(),
    )
    return jax.shard_map(
        coupled_step,
        mesh=mesh,
        in_specs=placed,
        out_specs=P(None, None, "lat", "lon"),
        check_vma=False,
    )
```

```python
import jax
import jax.numpy as jnp
from jax import lax
from jax.sharding import PartitionSpec as P


NSUB = 4


diffusion_number = 0.2


def shifted_pairs(count, step, wrap):
    pairs = []
    for i in range(count):
        j = i + step
        if 0 <= j < count:
            pairs.append((i, j))
        elif wrap:
            pairs.append((i, j % count))
    return pairs


def with_halo(block, width):
    lon_count = lax.axis_size("lon")
    lat_count = lax.axis_size("lat")
    planes, rows, _ = block.shape
    west = lax.ppermute(
        block[..., -width:].reshape(planes, rows * width), "lon", shifted_pairs(lon_count, 1, True)
    )
    east = lax.ppermute(
        block[..., :width].reshape(planes, rows * width), "lon", shifted_pairs(lon_count, -1, True)
    )
    west = west.reshape(planes, rows, width)
    east = east.reshape(planes, rows, width)
    top = jnp.concatenate(
        [west[:, -width:, :], block[:, -width:, :], east[:, -width:, :]], axis=-1
    )
    bottom = jnp.concatenate(
        [west[:, :width, :], block[:, :width, :], east[:, :width, :]], axis=-1
    )
    south = lax.ppermute(top, "lat", shifted_pairs(lat_count, 1, False))
    north = lax.ppermute(bottom, "lat", shifted_pairs(lat_count, -1, False))
    middle = jnp.concatenate([west, block, east], axis=-1)
    return jnp.concatenate([south, middle, north], axis=-2)


def advect(tracer_now, east_speed, north_speed, sea_mask):
    mask_east = sea_mask[:, :-1] * sea_mask[:, 1:]
    east_flow = mask_east * (
        east_speed[:, :, :-1] * (tracer_now[..., :-1] + tracer_now[..., 1:]) * 0.5
        - diffusion_number * (tracer_now[..., 1:] - tracer_now[..., :-1])
    )
    mask_north = sea_mask[:-1, :] * sea_mask[1:, :]
    north_flow = mask_north * (
        north_speed[:, :-1, :] * (tracer_now[..., :-1, :] + tracer_now[..., 1:, :]) * 0.5
        - diffusion_number * (tracer_now[..., 1:, :] - tracer_now[..., :-1, :])
    )
    inner = tracer_now[..., 1:-1, 1:-1]
    return (
        inner
        + east_flow[..., 1:-1, :-1]
        - east_flow[..., 1:-1, 1:]
        + north_flow[..., :-1, 1:-1]
        - north_flow[..., 1:, 1:-1]
    )


def coupled_step(
    atm_fluxes,
    remap_weights,
    source_block,
    target_block,
    block_count,
    tracers,
    east_velocity,
    north_velocity,
    land_mask,
    coupling,
):
    field_count, cell_count = atm_fluxes.shape
    block_cells = remap_weights.shape[-1]
    tile_count = block_count.shape[1]
    slot_count = source_block.shape[1] // tile_count
    tracer_count, level_count, lat_rows, lon_cols = tracers.shape

    slot_ids = jnp.arange(tile_count * slot_count, dtype=jnp.int32)
    is_live = slot_ids % slot_count < jnp.repeat(block_count[0], slot_count)
    targets = jnp.where(is_live, target_block[0], -1).astype(jnp.float32)
    atm_blocks = atm_fluxes.reshape(field_count, cell_count // block_cells, block_cells)
    chosen = jnp.take(atm_blocks, source_block[0], axis=1)
    chosen = chosen.transpose(1, 0, 2).reshape(tile_count, slot_count, field_count, block_cells)
    zero_block = jnp.zeros((tile_count, field_count, block_cells), chosen.dtype)
    diagonal = []
    for k in range(slot_count):
        diagonal.append(
            jnp.concatenate(
                [chosen[:, k] if j == k else zero_block for j in range(slot_count)], axis=-1
            )
        )
    diagonal.append(jnp.zeros((tile_count, 8, slot_count * block_cells), chosen.dtype))
    lhs = jnp.concatenate(diagonal, axis=1)
    stacked_weights = remap_weights[0].reshape(tile_count, slot_count * block_cells, block_cells)
    product = jnp.einsum(
        "trb,tbc->trc", lhs, stacked_weights, preferred_element_type=jnp.float32
    )
    row_ids = jnp.arange(slot_count * field_count + 8)
    slot_of_row = row_ids // field_count
    live_rows = is_live.reshape(tile_count, slot_count)
    tgt_rows = targets.reshape(tile_count, slot_count)
    kept = jnp.zeros((tile_count, slot_count * field_count + 8), jnp.bool_)
    tail = jnp.zeros((tile_count, slot_count * field_count + 8), jnp.float32)
    for k in range(slot_count):
        kept = kept | ((slot_of_row == k)[None, :] & live_rows[:, k : k + 1])
        tail = jnp.where(
            (row_ids == slot_count * field_count + k)[None, :], tgt_rows[:, k : k + 1], tail
        )
    sent = jnp.where(
        (row_ids < slot_count * field_count)[None, :, None],
        jnp.where(kept[:, :, None], product, jnp.float32(0.0)),
        tail[:, :, None],
    )
    arrived = lax.all_to_all(sent, ("lat", "lon"), split_axis=0, concat_axis=0, tiled=True)
    landed = arrived[:, slot_count * field_count : slot_count * (field_count + 1), 0]
    arrived = arrived[:, : slot_count * field_count]

    sea_here = land_mask.astype(jnp.float32)
    planes = tracer_count * level_count
    stacked = jnp.concatenate(
        [
            tracers.reshape(planes, lat_rows, lon_cols),
            east_velocity,
            north_velocity,
            sea_here[None],
        ],
        axis=0,
    )
    wide = with_halo(stacked, NSUB)
    tracer_now = wide[:planes].reshape(tracer_count, level_count, lat_rows + 2 * NSUB, lon_cols + 2 * NSUB)
    east_wide = wide[planes : planes + level_count]
    north_wide = wide[planes + level_count : planes + 2 * level_count]
    mask_wide = wide[-1]
    for substep in range(NSUB):
        cut = substep
        end_r = lat_rows + 2 * NSUB - cut
        end_c = lon_cols + 2 * NSUB - cut
        tracer_now = advect(
            tracer_now,
            east_wide[:, cut:end_r, cut:end_c],
            north_wide[:, cut:end_r, cut:end_c],
            mask_wide[cut:end_r, cut:end_c],
        )

    arrived = arrived.reshape(tile_count * slot_count, field_count, block_cells)
    landed = landed.reshape(tile_count * slot_count)
    chooser = (landed[None, :] == jnp.arange(lat_rows, dtype=jnp.float32)[:, None]).astype(
        jnp.float32
    )
    ocean_flux = jnp.einsum(
        "rk,kfc->rfc", chooser, arrived, precision=lax.Precision.HIGHEST,
        preferred_element_type=jnp.float32,
    )
    source = jnp.einsum(
        "pf,ifj->pij", coupling, ocean_flux, precision=lax.Precision.HIGHEST
    ).reshape(tracer_count, level_count, lat_rows, lon_cols)
    return tracer_now + sea_here * source


def solution(mesh):
    placed = (
        P(None, ("lat", "lon")),
        P(("lat", "lon"), None, None, None),
        P(("lat", "lon"), None),
        P(("lat", "lon"), None),
        P(("lat", "lon"), None),
        P(None, None, "lat", "lon"),
        P(None, "lat", "lon"),
        P(None, "lat", "lon"),
        P("lat", "lon"),
        P(),
    )
    return jax.shard_map(
        coupled_step,
        mesh=mesh,
        in_specs=placed,
        out_specs=P(None, None, "lat", "lon"),
        check_vma=False,
    )
```

```python
import jax
import jax.numpy as jnp
from jax import lax
from jax.sharding import PartitionSpec as P


NSUB = 4


diffusion_number = 0.2


def shifted_pairs(count, step, wrap):
    pairs = []
    for i in range(count):
        j = i + step
        if 0 <= j < count:
            pairs.append((i, j))
        elif wrap:
            pairs.append((i, j % count))
    return pairs


def with_halo(block, width):
    lon_count = lax.axis_size("lon")
    lat_count = lax.axis_size("lat")
    parts = block
    rows, _ = parts[0].shape[-2:]
    planes = sum(p.shape[0] for p in parts)
    tall_rows = rows + 2 * width
    top_rows = jnp.concatenate([p[:, -width:, :] for p in parts], axis=0)
    bottom_rows = jnp.concatenate([p[:, :width, :] for p in parts], axis=0)
    south = lax.ppermute(top_rows, "lat", shifted_pairs(lat_count, 1, False))
    north = lax.ppermute(bottom_rows, "lat", shifted_pairs(lat_count, -1, False))
    block = jnp.concatenate(parts, axis=0)
    east_edge = jnp.concatenate(
        [south[..., -width:], block[..., -width:], north[..., -width:]], axis=1
    ).reshape(planes, tall_rows * width)
    west_edge = jnp.concatenate(
        [south[..., :width], block[..., :width], north[..., :width]], axis=1
    ).reshape(planes, tall_rows * width)
    west = lax.ppermute(east_edge, "lon", shifted_pairs(lon_count, 1, True))
    east = lax.ppermute(west_edge, "lon", shifted_pairs(lon_count, -1, True))
    tall = jnp.concatenate([south, block, north], axis=1)
    west = west.reshape(planes, tall_rows, width)
    east = east.reshape(planes, tall_rows, width)
    return jnp.concatenate([west, tall, east], axis=-1)


def advect(tracer_now, east_speed, north_speed, sea_mask):
    mask_east = sea_mask[:, :-1] * sea_mask[:, 1:]
    east_flow = mask_east * (
        east_speed[:, :, :-1] * (tracer_now[..., :-1] + tracer_now[..., 1:]) * 0.5
        - diffusion_number * (tracer_now[..., 1:] - tracer_now[..., :-1])
    )
    mask_north = sea_mask[:-1, :] * sea_mask[1:, :]
    north_flow = mask_north * (
        north_speed[:, :-1, :] * (tracer_now[..., :-1, :] + tracer_now[..., 1:, :]) * 0.5
        - diffusion_number * (tracer_now[..., 1:, :] - tracer_now[..., :-1, :])
    )
    inner = tracer_now[..., 1:-1, 1:-1]
    return (
        inner
        + east_flow[..., 1:-1, :-1]
        - east_flow[..., 1:-1, 1:]
        + north_flow[..., :-1, 1:-1]
        - north_flow[..., 1:, 1:-1]
    )


def coupled_step(
    atm_fluxes,
    remap_weights,
    source_block,
    target_block,
    block_count,
    tracers,
    east_velocity,
    north_velocity,
    land_mask,
    coupling,
):
    field_count, cell_count = atm_fluxes.shape
    block_cells = remap_weights.shape[-1]
    tile_count = block_count.shape[1]
    slot_count = source_block.shape[1] // tile_count
    tracer_count, level_count, lat_rows, lon_cols = tracers.shape

    slot_ids = jnp.arange(tile_count * slot_count, dtype=jnp.int32)
    is_live = slot_ids % slot_count < jnp.repeat(block_count[0], slot_count)
    targets = jnp.where(is_live, target_block[0], -1).astype(jnp.float32)
    atm_blocks = atm_fluxes.reshape(field_count, cell_count // block_cells, block_cells)
    chosen = jnp.take(atm_blocks, source_block[0], axis=1)
    chosen = chosen.transpose(1, 0, 2).reshape(tile_count, slot_count, field_count, block_cells)
    zero_block = jnp.zeros((tile_count, field_count, block_cells), chosen.dtype)
    diagonal = []
    for k in range(slot_count):
        diagonal.append(
            jnp.concatenate(
                [chosen[:, k] if j == k else zero_block for j in range(slot_count)], axis=-1
            )
        )
    diagonal.append(jnp.zeros((tile_count, 8, slot_count * block_cells), chosen.dtype))
    lhs = jnp.concatenate(diagonal, axis=1)
    stacked_weights = remap_weights[0].reshape(tile_count, slot_count * block_cells, block_cells)
    product = jnp.einsum("trb,tbc->trc", lhs, stacked_weights, preferred_element_type=jnp.float32)
    row_ids = jnp.arange(slot_count * field_count + 8)
    slot_of_row = row_ids // field_count
    live_rows = is_live.reshape(tile_count, slot_count)
    tgt_rows = targets.reshape(tile_count, slot_count)
    kept = jnp.zeros((tile_count, slot_count * field_count + 8), jnp.bool_)
    tail = jnp.zeros((tile_count, slot_count * field_count + 8), jnp.float32)
    for k in range(slot_count):
        kept = kept | ((slot_of_row == k)[None, :] & live_rows[:, k : k + 1])
        tail = jnp.where(
            (row_ids == slot_count * field_count + k)[None, :], tgt_rows[:, k : k + 1], tail
        )
    sent = jnp.where(
        (row_ids < slot_count * field_count)[None, :, None],
        jnp.where(kept[:, :, None], product, jnp.float32(0.0)),
        tail[:, :, None],
    )
    arrived = lax.all_to_all(sent, ("lat", "lon"), split_axis=0, concat_axis=0, tiled=True)
    landed = arrived[:, slot_count * field_count : slot_count * (field_count + 1), 0]
    arrived = arrived[:, : slot_count * field_count]

    sea_here = land_mask.astype(jnp.float32)
    planes = tracer_count * level_count
    stacked = [
        tracers.reshape(planes, lat_rows, lon_cols),
        east_velocity,
        north_velocity,
        sea_here[None],
    ]
    wide = with_halo(stacked, NSUB)
    tracer_now = wide[:planes].reshape(tracer_count, level_count, lat_rows + 2 * NSUB, lon_cols + 2 * NSUB)
    east_wide = wide[planes : planes + level_count]
    north_wide = wide[planes + level_count : planes + 2 * level_count]
    mask_wide = wide[-1]
    for substep in range(NSUB):
        cut = substep
        end_r = lat_rows + 2 * NSUB - cut
        end_c = lon_cols + 2 * NSUB - cut
        tracer_now = advect(
            tracer_now,
            east_wide[:, cut:end_r, cut:end_c],
            north_wide[:, cut:end_r, cut:end_c],
            mask_wide[cut:end_r, cut:end_c],
        )

    arrived = arrived.reshape(tile_count * slot_count, field_count, block_cells)
    landed = landed.reshape(tile_count * slot_count)
    chooser = (landed[None, :] == jnp.arange(lat_rows, dtype=jnp.float32)[:, None]).astype(
        jnp.float32
    )
    ocean_flux = jnp.einsum(
        "rk,kfc->rfc", chooser, arrived, precision=lax.Precision.HIGHEST,
        preferred_element_type=jnp.float32,
    )
    source = jnp.einsum(
        "pf,ifj->pij", coupling, ocean_flux, precision=lax.Precision.HIGHEST
    ).reshape(tracer_count, level_count, lat_rows, lon_cols)
    return tracer_now + sea_here * source


def solution(mesh):
    placed = (
        P(None, ("lat", "lon")),
        P(("lat", "lon"), None, None, None),
        P(("lat", "lon"), None),
        P(("lat", "lon"), None),
        P(("lat", "lon"), None),
        P(None, None, "lat", "lon"),
        P(None, "lat", "lon"),
        P(None, "lat", "lon"),
        P("lat", "lon"),
        P(),
    )
    return jax.shard_map(
        coupled_step,
        mesh=mesh,
        in_specs=placed,
        out_specs=P(None, None, "lat", "lon"),
        check_vma=False,
    )
```

```python
import jax
import jax.numpy as jnp
from jax import lax
from jax.sharding import PartitionSpec as P


NSUB = 4


diffusion_number = 0.2


def shifted_pairs(count, step, wrap):
    pairs = []
    for i in range(count):
        j = i + step
        if 0 <= j < count:
            pairs.append((i, j))
        elif wrap:
            pairs.append((i, j % count))
    return pairs


def with_halo(block, width):
    lon_count = lax.axis_size("lon")
    lat_count = lax.axis_size("lat")
    planes, rows, _ = block.shape
    tall_rows = rows + 2 * width
    south = lax.ppermute(block[:, -width:, :], "lat", shifted_pairs(lat_count, 1, False))
    north = lax.ppermute(block[:, :width, :], "lat", shifted_pairs(lat_count, -1, False))
    east_edge = jnp.concatenate(
        [south[..., -width:], block[..., -width:], north[..., -width:]], axis=1
    ).reshape(planes, tall_rows * width)
    west_edge = jnp.concatenate(
        [south[..., :width], block[..., :width], north[..., :width]], axis=1
    ).reshape(planes, tall_rows * width)
    west = lax.ppermute(east_edge, "lon", shifted_pairs(lon_count, 1, True))
    east = lax.ppermute(west_edge, "lon", shifted_pairs(lon_count, -1, True))
    tall = jnp.concatenate([south, block, north], axis=1)
    west = west.reshape(planes, tall_rows, width)
    east = east.reshape(planes, tall_rows, width)
    return jnp.concatenate([west, tall, east], axis=-1)


def advect(tracer_now, east_speed, north_speed, sea_mask):
    mask_east = sea_mask[:, :-1] * sea_mask[:, 1:]
    east_flow = mask_east * (
        east_speed[:, :, :-1] * (tracer_now[..., :-1] + tracer_now[..., 1:]) * 0.5
        - diffusion_number * (tracer_now[..., 1:] - tracer_now[..., :-1])
    )
    mask_north = sea_mask[:-1, :] * sea_mask[1:, :]
    north_flow = mask_north * (
        north_speed[:, :-1, :] * (tracer_now[..., :-1, :] + tracer_now[..., 1:, :]) * 0.5
        - diffusion_number * (tracer_now[..., 1:, :] - tracer_now[..., :-1, :])
    )
    inner = tracer_now[..., 1:-1, 1:-1]
    return (
        inner
        + east_flow[..., 1:-1, :-1]
        - east_flow[..., 1:-1, 1:]
        + north_flow[..., :-1, 1:-1]
        - north_flow[..., 1:, 1:-1]
    )


def coupled_step(
    atm_fluxes,
    remap_weights,
    source_block,
    target_block,
    block_count,
    tracers,
    east_velocity,
    north_velocity,
    land_mask,
    coupling,
):
    field_count, cell_count = atm_fluxes.shape
    block_cells = remap_weights.shape[-1]
    tile_count = block_count.shape[1]
    slot_count = source_block.shape[1] // tile_count
    tracer_count, level_count, lat_rows, lon_cols = tracers.shape

    slot_ids = jnp.arange(tile_count * slot_count, dtype=jnp.int32)
    is_live = slot_ids % slot_count < jnp.repeat(block_count[0], slot_count)
    targets = jnp.where(is_live, target_block[0], -1).astype(jnp.float32)
    atm_blocks = atm_fluxes.reshape(field_count, cell_count // block_cells, block_cells)
    chosen = jnp.take(atm_blocks, source_block[0], axis=1)
    chosen = chosen.transpose(1, 0, 2).reshape(tile_count, slot_count, field_count, block_cells)
    zero_block = jnp.zeros((tile_count, field_count, block_cells), chosen.dtype)
    diagonal = []
    for k in range(slot_count):
        diagonal.append(
            jnp.concatenate(
                [chosen[:, k] if j == k else zero_block for j in range(slot_count)], axis=-1
            )
        )
    diagonal.append(jnp.zeros((tile_count, 8, slot_count * block_cells), chosen.dtype))
    lhs = jnp.concatenate(diagonal, axis=1)
    stacked_weights = remap_weights[0].reshape(tile_count, slot_count * block_cells, block_cells)
    product = jnp.einsum("trb,tbc->trc", lhs, stacked_weights, preferred_element_type=jnp.float32)
    row_ids = jnp.arange(slot_count * field_count + 8)
    slot_of_row = row_ids // field_count
    live_rows = is_live.reshape(tile_count, slot_count)
    tgt_rows = targets.reshape(tile_count, slot_count)
    kept = jnp.zeros((tile_count, slot_count * field_count + 8), jnp.bool_)
    tail = jnp.zeros((tile_count, slot_count * field_count + 8), jnp.float32)
    for k in range(slot_count):
        kept = kept | ((slot_of_row == k)[None, :] & live_rows[:, k : k + 1])
        tail = jnp.where(
            (row_ids == slot_count * field_count + k)[None, :], tgt_rows[:, k : k + 1], tail
        )
    sent = jnp.where(
        (row_ids < slot_count * field_count)[None, :, None],
        jnp.where(kept[:, :, None], product, jnp.float32(0.0)),
        tail[:, :, None],
    )
    arrived = lax.all_to_all(sent, ("lat", "lon"), split_axis=0, concat_axis=0, tiled=True)
    landed = arrived[:, slot_count * field_count : slot_count * (field_count + 1), 0]
    arrived = arrived[:, : slot_count * field_count]

    sea_here = land_mask.astype(jnp.float32)
    planes = tracer_count * level_count
    stacked = jnp.concatenate(
        [
            tracers.reshape(planes, lat_rows, lon_cols),
            east_velocity,
            north_velocity,
            sea_here[None],
        ],
        axis=0,
    )
    wide = with_halo(stacked, NSUB)
    tracer_now = wide[:planes].reshape(tracer_count, level_count, lat_rows + 2 * NSUB, lon_cols + 2 * NSUB)
    east_wide = wide[planes : planes + level_count]
    north_wide = wide[planes + level_count : planes + 2 * level_count]
    mask_wide = wide[-1]
    for substep in range(NSUB):
        cut = substep
        end_r = lat_rows + 2 * NSUB - cut
        end_c = lon_cols + 2 * NSUB - cut
        tracer_now = advect(
            tracer_now,
            east_wide[:, cut:end_r, cut:end_c],
            north_wide[:, cut:end_r, cut:end_c],
            mask_wide[cut:end_r, cut:end_c],
        )

    arrived = arrived.reshape(tile_count * slot_count, field_count, block_cells)
    landed = landed.reshape(tile_count * slot_count)
    chooser = (landed[None, :] == jnp.arange(lat_rows, dtype=jnp.float32)[:, None]).astype(
        jnp.float32
    )
    ocean_flux = jnp.einsum(
        "rk,kfc->rfc", chooser, arrived, precision=lax.Precision.HIGH,
        preferred_element_type=jnp.float32,
    )
    source = jnp.einsum(
        "pf,ifj->pij", coupling, ocean_flux, precision=lax.Precision.HIGH
    ).reshape(tracer_count, level_count, lat_rows, lon_cols)
    return tracer_now + sea_here * source


def solution(mesh):
    placed = (
        P(None, ("lat", "lon")),
        P(("lat", "lon"), None, None, None),
        P(("lat", "lon"), None),
        P(("lat", "lon"), None),
        P(("lat", "lon"), None),
        P(None, None, "lat", "lon"),
        P(None, "lat", "lon"),
        P(None, "lat", "lon"),
        P("lat", "lon"),
        P(),
    )
    return jax.shard_map(
        coupled_step,
        mesh=mesh,
        in_specs=placed,
        out_specs=P(None, None, "lat", "lon"),
        check_vma=False,
    )
```
